32 devices in a mesh: grp: 4 (over y, x), box: 8 (over z, core).
Axes of the slice: x: 2, y: 2, z: 4, core: 2. Of those that a mesh axis runs over, the one named last changes fastest.
Arguments:
- leaf_maps: float32 [4, 8, 1024, 1024], P('grp', 'box'), may hold values from -4 to 30
- side_points: int32 [4, 8, 4, 256], P('grp', 'box'), may hold values from 0 to 1023, as said below
Outputs:
- merged_rows: float32 [4, 8, 512, 2048], P('grp', 'box')
The draws below stay inside these ranges and needn't reach their ends.
Inputs may be any that keep to these rules, and one draw needn't show every extreme that they name: `side_points`: for each leaf box, its four lists of 256 indices together name each of the 1024 rows of its map exactly once.
All inputs are finite; a program needn't handle non-finite values.
Results may differ from the reference program's by a relative error of at most 0.0001.
Values sent between devices are 32-bit elements; how exact they have to be, the bound alone decides.
No kernel may reach another device: no remote copies, remote signals or barrier semaphores. Data moves between devices by JAX's collectives and lax.ppermute only.
A program may use at most 64 MiB of HBM per device.

```python
import math
import jax
import jax.numpy as jnp
from jax import lax

Q = 256
ITERS_LOW = 3
ITERS_HIGH = 3
GROUPS = 4
BOXES = 8


def box_orders(key):
    box_count = GROUPS * BOXES
    box_keys = jax.random.split(jax.random.fold_in(key, 11), box_count)
    return jax.vmap(lambda one_key: jax.random.permutation(one_key, 4 * Q))(box_keys).astype(jnp.int32)


def draw_side_points(key, part):
    return box_orders(key).reshape(GROUPS, BOXES, 4, Q)


def draw_leaf_maps(key, part):
    box_count = GROUPS * BOXES
    orders = box_orders(key)
    box_keys = jax.random.split(jax.random.fold_in(key, 23), box_count)
    side_of = jnp.arange(4 * Q) // Q
    same_side = side_of[:, None] == side_of[None, :]
    spread = jnp.where(same_side, 12.8, 16.0) / math.sqrt(Q)
    identity = jnp.eye(4 * Q, dtype=jnp.float32)

    def one_box(box_item):
        box_key, point_order = box_item
        noise_key, diagonal_key = jax.random.split(box_key)
        noise_field = jax.random.truncated_normal(noise_key, -4.0, 4.0, (4 * Q, 4 * Q), jnp.float32)
        diagonal = jax.random.uniform(diagonal_key, (4 * Q,), jnp.float32, 20.0, 30.0)
        side_map = noise_field * spread * (1.0 - identity) + identity * diagonal[None, :]
        blank_map = jnp.zeros((4 * Q, 4 * Q), jnp.float32)
        return blank_map.at[point_order[:, None], point_order[None, :]].set(side_map)
    return lax.map(one_box, (box_keys, orders)).reshape(GROUPS, BOXES, 4 * Q, 4 * Q)


def setup_inputs(seed: int = 0) -> dict:
    arg_keys = jax.random.split(jax.random.key(seed), 3)
    leaf_maps = draw_leaf_maps(jax.random.fold_in(arg_keys[2], 71), 0)
    side_points = draw_side_points(jax.random.fold_in(arg_keys[2], 71), 0)
    return dict(leaf_maps=leaf_maps, side_points=side_points)


def matmul(left, right):
    return jnp.dot(left, right, precision=lax.Precision.HIGHEST, preferred_element_type=jnp.float32)


def newton(system, steps):
    inverse = jnp.diag(1.0 / jnp.diagonal(system))
    for sweep_index in range(steps):
        inverse = 2.0 * inverse - matmul(matmul(inverse, system), inverse)
    return inverse


def select_block(matrix, row_index, col_index):
    return jnp.take(jnp.take(matrix, row_index, axis=0), col_index, axis=1)


def block_index(blocks):
    return jnp.concatenate([jnp.arange(k * Q, (k + 1) * Q, dtype=jnp.int32) for k in blocks])


def merge_pair(pair_item):
    pair_maps, pair_sides = pair_item
    left_map, right_map = pair_maps[0], pair_maps[1]
    left_sides, right_sides = pair_sides[0], pair_sides[1]
    left_ext = jnp.concatenate([left_sides[0], left_sides[2], left_sides[3]])
    left_int = left_sides[1]
    right_ext = jnp.concatenate([right_sides[1], right_sides[2], right_sides[3]])
    right_int = right_sides[0]
    system = select_block(left_map, left_int, left_int) + select_block(right_map, right_int, right_int)
    inverse = newton(system, ITERS_LOW)
    coupling = jnp.concatenate([select_block(left_map, left_int, left_ext), select_block(right_map, right_int, right_ext)], 1)
    solved = -matmul(inverse, coupling)
    blank_block = jnp.zeros((3 * Q, 3 * Q), jnp.float32)
    top_rows = jnp.concatenate([select_block(left_map, left_ext, left_ext), blank_block], 1) + matmul(select_block(left_map, left_ext, left_int), solved)
    bottom_rows = jnp.concatenate([blank_block, select_block(right_map, right_ext, right_ext)], 1) + matmul(select_block(right_map, right_ext, right_int), solved)
    return jnp.concatenate([top_rows, bottom_rows], 0)


def merge_quad(parents):
    lower_map, upper_map = parents[0], parents[1]
    lower_ext = block_index([0, 1, 3, 4])
    lower_int = block_index([2, 5])
    upper_ext = block_index([0, 2, 3, 5])
    upper_int = block_index([1, 4])
    system = select_block(lower_map, lower_int, lower_int) + select_block(upper_map, upper_int, upper_int)
    inverse = newton(system, ITERS_HIGH)
    coupling = jnp.concatenate([select_block(lower_map, lower_int, lower_ext), select_block(upper_map, upper_int, upper_ext)], 1)
    solved = -matmul(inverse, coupling)
    blank_block = jnp.zeros((4 * Q, 4 * Q), jnp.float32)
    top_rows = jnp.concatenate([select_block(lower_map, lower_ext, lower_ext), blank_block], 1) + matmul(select_block(lower_map, lower_ext, lower_int), solved)
    bottom_rows = jnp.concatenate([blank_block, select_block(upper_map, upper_ext, upper_ext)], 1) + matmul(select_block(upper_map, upper_ext, upper_int), solved)
    return jnp.concatenate([top_rows, bottom_rows], 0)


def reference(leaf_maps, side_points):
    half_g = GROUPS // 2
    half_b = BOXES // 2
    pair_maps = leaf_maps.reshape(GROUPS, 2, half_b, 4 * Q, 4 * Q).transpose(0, 2, 1, 3, 4)
    pair_maps = pair_maps.reshape(GROUPS * half_b, 2, 4 * Q, 4 * Q)
    pair_sides = side_points.reshape(GROUPS, 2, half_b, 4, Q).transpose(0, 2, 1, 3, 4)
    pair_sides = pair_sides.reshape(GROUPS * half_b, 2, 4, Q)
    parents = lax.map(merge_pair, (pair_maps, pair_sides))
    parents = parents.reshape(2, half_g, half_b, 6 * Q, 6 * Q).transpose(1, 2, 0, 3, 4)
    parents = parents.reshape(half_g * half_b, 2, 6 * Q, 6 * Q)
    merged = lax.map(merge_quad, parents)
    merged = merged.reshape(half_g, half_b, 2, 2, 2 * Q, 8 * Q).transpose(2, 0, 3, 1, 4, 5)
    return merged.reshape(GROUPS, BOXES, 2 * Q, 8 * Q)
```

```python
import jax
import jax.numpy as jnp
from jax import lax
from jax.sharding import PartitionSpec as P

ITERS_LOW = 3
ITERS_HIGH = 3


def matmul(left, right):
    return jnp.dot(left, right, precision=lax.Precision.HIGHEST, preferred_element_type=jnp.float32)


def newton(system, steps):
    recip = 1.0 / jnp.diagonal(system)
    size = system.shape[0]
    eye = jnp.eye(size, dtype=jnp.float32)
    inverse = 2.0 * eye * recip[None, :] - recip[:, None] * system * recip[None, :]
    for sweep_index in range(steps - 1):
        inverse = 2.0 * inverse - matmul(matmul(inverse, system), inverse)
    return inverse


def swap(value, axis):
    size = lax.axis_size(axis)
    half = size // 2
    pairs = [(source, (source + half) % size) for source in range(size)]
    return lax.ppermute(value, axis, pairs)


def pair_solve(first_i1, second_i1, width):
    system = first_i1[:, :width] + second_i1[:, :width]
    inverse = newton(system, ITERS_LOW)
    coupling = jnp.concatenate([first_i1[:, width:], second_i1[:, width:]], 1)
    return -matmul(inverse, coupling)


def first_rows(rows, solved, width):
    blank = jnp.zeros((rows.shape[0], 3 * width), jnp.float32)
    return jnp.concatenate([rows[:, width:], blank], 1) + matmul(rows[:, :width], solved)


def second_rows(rows, solved, width):
    blank = jnp.zeros((rows.shape[0], 3 * width), jnp.float32)
    return jnp.concatenate([blank, rows[:, width:]], 1) + matmul(rows[:, :width], solved)


def ext_cols(parent, width):
    return jnp.concatenate(
        [parent[:, 0 : 2 * width], parent[:, 3 * width : 5 * width]], 1
    )


def int_cols(parent, width):
    return jnp.concatenate(
        [parent[:, 2 * width : 3 * width], parent[:, 5 * width : 6 * width]], 1
    )


def body(leaf_maps, side_points):
    upper = lax.axis_index("grp") // (lax.axis_size("grp") // 2)
    right = lax.axis_index("box") // (lax.axis_size("box") // 2)
    leaf = leaf_maps[0, 0]
    side_lists = side_points[0, 0]
    width = side_lists.shape[1]
    order = jnp.stack([1 - right, right, 2 + upper, 3 - upper])
    perm = jnp.take(side_lists, order, axis=0).reshape(4 * width)
    own_i1 = jnp.take(jnp.take(leaf, perm[:width], axis=0), perm, axis=1)
    own_i2 = jnp.take(jnp.take(leaf, perm[3 * width :], axis=0), perm, axis=1)
    own_ov = jnp.take(jnp.take(leaf, perm[width : 3 * width], axis=0), perm, axis=1)

    side_i1 = swap(own_i1, "box")
    side_i2 = swap(own_i2, "box")
    vert_i1 = swap(own_i1, "grp")
    vert_i2 = swap(own_i2, "grp")
    diag_i1 = swap(side_i1, "grp")
    diag_i2 = swap(side_i2, "grp")

    solved_own = pair_solve(own_i1, side_i1, width)
    own_ext = first_rows(own_ov, solved_own, width)
    own_int = first_rows(own_i2, solved_own, width)
    side_int = second_rows(side_i2, solved_own, width)

    solved_other = pair_solve(vert_i1, diag_i1, width)
    vert_int = first_rows(vert_i2, solved_other, width)
    diag_int = second_rows(diag_i2, solved_other, width)

    near = jnp.concatenate([own_int, side_int], 0)
    far = jnp.concatenate([vert_int, diag_int], 0)
    system_two = int_cols(near, width) + int_cols(far, width)
    inverse_two = newton(system_two, ITERS_HIGH)
    coupling_two = jnp.concatenate([ext_cols(near, width), ext_cols(far, width)], 1)
    weights = matmul(int_cols(own_ext, width), inverse_two)
    blank_wide = jnp.zeros((2 * width, 4 * width), jnp.float32)
    merged = jnp.concatenate([ext_cols(own_ext, width), blank_wide], 1) - matmul(weights, coupling_two)

    own_id = 2 * upper + right
    block_ids = jnp.bitwise_xor(jnp.arange(4, dtype=jnp.int32), own_id)
    merged = jnp.take(merged.reshape(2 * width, 4, 2 * width), block_ids, axis=1)
    return merged.reshape(2 * width, 8 * width)[None, None]


def solution(mesh):
    in_specs = (P("grp", "box", None, None), P("grp", "box", None, None))
    out_specs = P("grp", "box", None, None)
    return jax.shard_map(body, mesh=mesh, in_specs=in_specs, out_specs=out_specs, check_vma=False)
```

```python
import jax
import jax.numpy as jnp
from jax import lax
from jax.sharding import PartitionSpec as P

ITERS_LOW = 3
ITERS_HIGH = 3


def matmul(left, right):
    return jnp.dot(left, right, precision=lax.Precision.HIGHEST, preferred_element_type=jnp.float32)


def newton(system, steps):
    recip = 1.0 / jnp.diagonal(system)
    size = system.shape[0]
    eye = jnp.eye(size, dtype=jnp.float32)
    inverse = 2.0 * eye * recip[None, :] - recip[:, None] * system * recip[None, :]
    for sweep_index in range(steps - 1):
        inverse = 2.0 * inverse - matmul(matmul(inverse, system), inverse)
    return inverse


def swap(value, axis):
    size = lax.axis_size(axis)
    half = size // 2
    pairs = [(source, (source + half) % size) for source in range(size)]
    return lax.ppermute(value, axis, pairs)


def pair_solve(first_i1, second_i1, width):
    system = first_i1[:, :width] + second_i1[:, :width]
    inverse = newton(system, ITERS_LOW)
    coupling = jnp.concatenate([first_i1[:, width:], second_i1[:, width:]], 1)
    return -matmul(inverse, coupling)


def first_rows(rows, solved, width):
    blank = jnp.zeros((rows.shape[0], 3 * width), jnp.float32)
    return jnp.concatenate([rows[:, width:], blank], 1) + matmul(rows[:, :width], solved)


def second_rows(rows, solved, width):
    blank = jnp.zeros((rows.shape[0], 3 * width), jnp.float32)
    return jnp.concatenate([blank, rows[:, width:]], 1) + matmul(rows[:, :width], solved)


def ext_cols(parent, width):
    return jnp.concatenate(
        [parent[:, 0 : 2 * width], parent[:, 3 * width : 5 * width]], 1
    )


def int_cols(parent, width):
    return jnp.concatenate(
        [parent[:, 2 * width : 3 * width], parent[:, 5 * width : 6 * width]], 1
    )


def body(leaf_maps, side_points):
    upper = lax.axis_index("grp") // (lax.axis_size("grp") // 2)
    right = lax.axis_index("box") // (lax.axis_size("box") // 2)
    leaf = leaf_maps[0, 0]
    side_lists = side_points[0, 0]
    width = side_lists.shape[1]
    order = jnp.stack([1 - right, right, 2 + upper, 3 - upper])
    perm = jnp.take(side_lists, order, axis=0).reshape(4 * width)
    own_i1 = jnp.take(jnp.take(leaf, perm[:width], axis=0), perm, axis=1)
    own_i2 = jnp.take(jnp.take(leaf, perm[3 * width :], axis=0), perm, axis=1)
    own_ov = jnp.take(jnp.take(leaf, perm[width : 3 * width], axis=0), perm, axis=1)

    half = width // 2
    vert_i1 = swap(own_i1, "grp")
    vert_i2 = swap(own_i2, "grp")
    side_i1 = swap(own_i1, "box")
    diag_i1 = swap(side_i1, "grp")
    first_half, side_i1 = lax.optimization_barrier((own_i2[:half], side_i1))
    side_first = swap(first_half, "box")
    diag_first = swap(side_first, "grp")
    second_half, side_first = lax.optimization_barrier((own_i2[half:], side_first))
    side_second = swap(second_half, "box")
    diag_second = swap(side_second, "grp")
    side_i2 = jnp.concatenate([side_first, side_second], 0)
    diag_i2 = jnp.concatenate([diag_first, diag_second], 0)

    solved_own = pair_solve(own_i1, side_i1, width)
    own_ext = first_rows(own_ov, solved_own, width)
    own_int = first_rows(own_i2, solved_own, width)
    side_int = second_rows(side_i2, solved_own, width)

    solved_other = pair_solve(vert_i1, diag_i1, width)
    vert_int = first_rows(vert_i2, solved_other, width)
    diag_int = second_rows(diag_i2, solved_other, width)

    near = jnp.concatenate([own_int, side_int], 0)
    far = jnp.concatenate([vert_int, diag_int], 0)
    system_two = int_cols(near, width) + int_cols(far, width)
    inverse_two = newton(system_two, ITERS_HIGH)
    weights = matmul(int_cols(own_ext, width), inverse_two)
    own_id = 2 * upper + right
    pieces = [
        own_ext[:, 0 : 2 * width] - matmul(weights, near[:, 0 : 2 * width]),
        own_ext[:, 3 * width : 5 * width] - matmul(weights, near[:, 3 * width : 5 * width]),
        -matmul(weights, far[:, 0 : 2 * width]),
        -matmul(weights, far[:, 3 * width : 5 * width]),
    ]
    merged = jnp.zeros((2 * width, 8 * width), jnp.float32)
    for rel, piece in enumerate(pieces):
        start = jnp.bitwise_xor(own_id, rel) * (2 * width)
        merged = lax.dynamic_update_slice(merged, piece, (0, start))
    return merged[None, None]


def solution(mesh):
    in_specs = (P("grp", "box", None, None), P("grp", "box", None, None))
    out_specs = P("grp", "box", None, None)
    return jax.shard_map(body, mesh=mesh, in_specs=in_specs, out_specs=out_specs, check_vma=False)
```

```python
import jax
import jax.numpy as jnp
from jax import lax
from jax.sharding import PartitionSpec as P

ITERS_LOW = 3
ITERS_HIGH = 3


def matmul(left, right):
    return jnp.dot(left, right, precision=lax.Precision.HIGHEST, preferred_element_type=jnp.float32)


def newton(system, steps):
    size = system.shape[0]
    eye = jnp.eye(size, dtype=jnp.float32)
    recip = 1.0 / jnp.sum(jnp.where(eye > 0, system, 0.0), axis=1)
    inverse = 2.0 * eye * recip[None, :] - recip[:, None] * system * recip[None, :]
    for sweep_index in range(steps - 1):
        inverse = 2.0 * inverse - matmul(matmul(inverse, system), inverse)
    return inverse


def swap(value, axis):
    size = lax.axis_size(axis)
    half = size // 2
    pairs = [(source, (source + half) % size) for source in range(size)]
    return lax.ppermute(value, axis, pairs)


def pair_solve(first_i1, second_i1, width):
    system = first_i1[:, :width] + second_i1[:, :width]
    inverse = newton(system, ITERS_LOW)
    coupling = jnp.concatenate([first_i1[:, width:], second_i1[:, width:]], 1)
    return -matmul(inverse, coupling)


def first_rows(rows, solved, width):
    blank = jnp.zeros((rows.shape[0], 3 * width), jnp.float32)
    return jnp.concatenate([rows[:, width:], blank], 1) + matmul(rows[:, :width], solved)


def second_rows(rows, solved, width):
    blank = jnp.zeros((rows.shape[0], 3 * width), jnp.float32)
    return jnp.concatenate([blank, rows[:, width:]], 1) + matmul(rows[:, :width], solved)


def ext_cols(parent, width):
    return jnp.concatenate(
        [parent[:, 0 : 2 * width], parent[:, 3 * width : 5 * width]], 1
    )


def int_cols(parent, width):
    return jnp.concatenate(
        [parent[:, 2 * width : 3 * width], parent[:, 5 * width : 6 * width]], 1
    )


def pick(matrix, rows, cols):
    picked = jnp.take(matrix, rows, axis=0, mode="clip")
    return jnp.take(picked, cols, axis=1, mode="clip")


def body(leaf_maps, side_points):
    upper = lax.axis_index("grp") // (lax.axis_size("grp") // 2)
    right = lax.axis_index("box") // (lax.axis_size("box") // 2)
    leaf = leaf_maps[0, 0]
    side_lists = side_points[0, 0]
    width = side_lists.shape[1]
    order = jnp.stack([1 - right, right, 2 + upper, 3 - upper])
    perm = jnp.take(side_lists, order, axis=0, mode="clip").reshape(4 * width)
    own_i1 = pick(leaf, perm[:width], perm)
    leaf, own_i1 = lax.optimization_barrier((leaf, own_i1))
    own_i2 = pick(leaf, perm[3 * width :], perm)
    own_ov = pick(leaf, perm[width : 3 * width], perm)

    half = width // 2
    vert_i1 = swap(own_i1, "grp")
    vert_i2 = swap(own_i2, "grp")
    side_i1 = swap(own_i1, "box")
    diag_i1 = swap(side_i1, "grp")
    first_half, side_i1 = lax.optimization_barrier((own_i2[:half], side_i1))
    side_first = swap(first_half, "box")
    diag_first = swap(side_first, "grp")
    second_half, side_first = lax.optimization_barrier((own_i2[half:], side_first))
    side_second = swap(second_half, "box")
    diag_second = swap(side_second, "grp")
    side_i2 = jnp.concatenate([side_first, side_second], 0)
    diag_i2 = jnp.concatenate([diag_first, diag_second], 0)

    solved_own = pair_solve(own_i1, side_i1, width)
    own_ext = first_rows(own_ov, solved_own, width)
    own_int = first_rows(own_i2, solved_own, width)
    side_int = second_rows(side_i2, solved_own, width)

    solved_other = pair_solve(vert_i1, diag_i1, width)
    vert_int = first_rows(vert_i2, solved_other, width)
    diag_int = second_rows(diag_i2, solved_other, width)

    near = jnp.concatenate([own_int, side_int], 0)
    far = jnp.concatenate([vert_int, diag_int], 0)
    system_two = int_cols(near, width) + int_cols(far, width)
    inverse_two = newton(system_two, ITERS_HIGH)
    weights = matmul(int_cols(own_ext, width), inverse_two)
    own_id = 2 * upper + right
    pieces = [
        own_ext[:, 0 : 2 * width] - matmul(weights, near[:, 0 : 2 * width]),
        own_ext[:, 3 * width : 5 * width] - matmul(weights, near[:, 3 * width : 5 * width]),
        -matmul(weights, far[:, 0 : 2 * width]),
        -matmul(weights, far[:, 3 * width : 5 * width]),
    ]
    merged = jnp.zeros((2 * width, 8 * width), jnp.float32)
    for rel, piece in enumerate(pieces):
        start = jnp.bitwise_xor(own_id, rel) * (2 * width)
        merged = lax.dynamic_update_slice(merged, piece, (0, start))
    return merged[None, None]


def solution(mesh):
    in_specs = (P("grp", "box", None, None), P("grp", "box", None, None))
    out_specs = P("grp", "box", None, None)
    return jax.shard_map(body, mesh=mesh, in_specs=in_specs, out_specs=out_specs, check_vma=False)
```

```python
import jax
import jax.numpy as jnp
from jax import lax
from jax.sharding import PartitionSpec as P

ITERS_LOW = 3
ITERS_HIGH = 3


def matmul(left, right):
    return jnp.dot(left, right, precision=lax.Precision.HIGHEST, preferred_element_type=jnp.float32)


def matmul_high(left, right):
    return jnp.dot(left, right, precision=lax.Precision.HIGH, preferred_element_type=jnp.float32)


def newton(system, steps, product=matmul):
    size = system.shape[0]
    eye = jnp.eye(size, dtype=jnp.float32)
    recip = 1.0 / jnp.sum(jnp.where(eye > 0, system, 0.0), axis=1)
    inverse = 2.0 * eye * recip[None, :] - recip[:, None] * system * recip[None, :]
    for sweep_index in range(steps - 1):
        inverse = 2.0 * inverse - product(product(inverse, system), inverse)
    return inverse


def swap(value, axis):
    size = lax.axis_size(axis)
    half = size // 2
    pairs = [(source, (source + half) % size) for source in range(size)]
    return lax.ppermute(value, axis, pairs)


def pair_solve(first_i1, second_i1, width):
    system = first_i1[:, :width] + second_i1[:, :width]
    inverse = newton(system, ITERS_LOW)
    coupling = jnp.concatenate([first_i1[:, width:], second_i1[:, width:]], 1)
    return -matmul(inverse, coupling)


def first_rows(rows, solved, width):
    blank = jnp.zeros((rows.shape[0], 3 * width), jnp.float32)
    return jnp.concatenate([rows[:, width:], blank], 1) + matmul(rows[:, :width], solved)


def second_rows(rows, solved, width):
    blank = jnp.zeros((rows.shape[0], 3 * width), jnp.float32)
    return jnp.concatenate([blank, rows[:, width:]], 1) + matmul(rows[:, :width], solved)


def ext_cols(parent, width):
    return jnp.concatenate(
        [parent[:, 0 : 2 * width], parent[:, 3 * width : 5 * width]], 1
    )


def int_cols(parent, width):
    return jnp.concatenate(
        [parent[:, 2 * width : 3 * width], parent[:, 5 * width : 6 * width]], 1
    )


def pick(matrix, rows, cols):
    picked = jnp.take(matrix, rows, axis=0, mode="clip")
    return jnp.take(picked, cols, axis=1, mode="clip")


def body(leaf_maps, side_points):
    upper = lax.axis_index("grp") // (lax.axis_size("grp") // 2)
    right = lax.axis_index("box") // (lax.axis_size("box") // 2)
    leaf = leaf_maps[0, 0]
    side_lists = side_points[0, 0]
    width = side_lists.shape[1]
    order = jnp.stack([1 - right, right, 2 + upper, 3 - upper])
    perm = jnp.take(side_lists, order, axis=0, mode="clip").reshape(4 * width)
    own_i1 = pick(leaf, perm[:width], perm)
    leaf, own_i1 = lax.optimization_barrier((leaf, own_i1))
    own_i2 = pick(leaf, perm[3 * width :], perm)
    own_ov = pick(leaf, perm[width : 3 * width], perm)

    half = width // 2
    vert_i1 = swap(own_i1, "grp")
    vert_i2 = swap(own_i2, "grp")
    side_i1 = swap(own_i1, "box")
    diag_i1 = swap(side_i1, "grp")
    first_half, side_i1 = lax.optimization_barrier((own_i2[:half], side_i1))
    side_first = swap(first_half, "box")
    diag_first = swap(side_first, "grp")
    second_half, side_first = lax.optimization_barrier((own_i2[half:], side_first))
    side_second = swap(second_half, "box")
    diag_second = swap(side_second, "grp")
    side_i2 = jnp.concatenate([side_first, side_second], 0)
    diag_i2 = jnp.concatenate([diag_first, diag_second], 0)

    solved_own = pair_solve(own_i1, side_i1, width)
    own_ext = first_rows(own_ov, solved_own, width)
    own_int = first_rows(own_i2, solved_own, width)
    side_int = second_rows(side_i2, solved_own, width)

    solved_other = pair_solve(vert_i1, diag_i1, width)
    vert_int = first_rows(vert_i2, solved_other, width)
    diag_int = second_rows(diag_i2, solved_other, width)

    near = jnp.concatenate([own_int, side_int], 0)
    far = jnp.concatenate([vert_int, diag_int], 0)
    system_two = int_cols(near, width) + int_cols(far, width)
    inverse_two = newton(system_two, ITERS_HIGH, matmul_high)
    weights = matmul_high(int_cols(own_ext, width), inverse_two)
    own_id = 2 * upper + right
    pieces = [
        own_ext[:, 0 : 2 * width] - matmul_high(weights, near[:, 0 : 2 * width]),
        own_ext[:, 3 * width : 5 * width] - matmul_high(weights, near[:, 3 * width : 5 * width]),
        -matmul_high(weights, far[:, 0 : 2 * width]),
        -matmul_high(weights, far[:, 3 * width : 5 * width]),
    ]
    merged = jnp.zeros((2 * width, 8 * width), jnp.float32)
    for rel, piece in enumerate(pieces):
        start = jnp.bitwise_xor(own_id, rel) * (2 * width)
        merged = lax.dynamic_update_slice(merged, piece, (0, start))
    return merged[None, None]


def solution(mesh):
    in_specs = (P("grp", "box", None, None), P("grp", "box", None, None))
    out_specs = P("grp", "box", None, None)
    return jax.shard_map(body, mesh=mesh, in_specs=in_specs, out_specs=out_specs, check_vma=False)
```

```python
import jax
import jax.numpy as jnp
from jax import lax
from jax.sharding import PartitionSpec as P

ITERS_LOW = 3
ITERS_HIGH = 3


def matmul(left, right):
    return jnp.dot(left, right, precision=lax.Precision.HIGHEST, preferred_element_type=jnp.float32)


def matmul_high(left, right):
    return jnp.dot(left, right, precision=lax.Precision.HIGH, preferred_element_type=jnp.float32)


def newton(system, steps, product=matmul):
    size = system.shape[0]
    eye = jnp.eye(size, dtype=jnp.float32)
    recip = 1.0 / jnp.sum(jnp.where(eye > 0, system, 0.0), axis=1)
    inverse = 2.0 * eye * recip[None, :] - recip[:, None] * system * recip[None, :]
    for sweep_index in range(steps - 1):
        inverse = 2.0 * inverse - product(product(inverse, system), inverse)
    return inverse


def swap(value, axis):
    size = lax.axis_size(axis)
    half = size // 2
    pairs = [(source, (source + half) % size) for source in range(size)]
    return lax.ppermute(value, axis, pairs)


def pair_solve(first_i1, second_i1, width):
    system = first_i1[:, :width] + second_i1[:, :width]
    inverse = newton(system, ITERS_LOW)
    coupling = jnp.concatenate([first_i1[:, width:], second_i1[:, width:]], 1)
    return -matmul(inverse, coupling)


def first_rows(rows, solved, width):
    blank = jnp.zeros((rows.shape[0], 3 * width), jnp.float32)
    return jnp.concatenate([rows[:, width:], blank], 1) + matmul(rows[:, :width], solved)


def second_rows(rows, solved, width):
    blank = jnp.zeros((rows.shape[0], 3 * width), jnp.float32)
    return jnp.concatenate([blank, rows[:, width:]], 1) + matmul(rows[:, :width], solved)


def ext_cols(parent, width):
    return jnp.concatenate(
        [parent[:, 0 : 2 * width], parent[:, 3 * width : 5 * width]], 1
    )


def int_cols(parent, width):
    return jnp.concatenate(
        [parent[:, 2 * width : 3 * width], parent[:, 5 * width : 6 * width]], 1
    )


def pick(matrix, rows, cols):
    picked = jnp.take(matrix, rows, axis=0, mode="clip")
    return jnp.take(picked, cols, axis=1, mode="clip")


def body(leaf_maps, side_points):
    upper = lax.axis_index("grp") // (lax.axis_size("grp") // 2)
    right = lax.axis_index("box") // (lax.axis_size("box") // 2)
    leaf = leaf_maps[0, 0]
    side_lists = side_points[0, 0]
    width = side_lists.shape[1]
    order = jnp.stack([1 - right, right, 2 + upper, 3 - upper])
    perm = jnp.take(side_lists, order, axis=0, mode="clip").reshape(4 * width)
    raw_i1 = jnp.take(leaf, perm[:width], axis=0, mode="clip")
    vert_raw = swap(raw_i1, "grp")
    side_raw = swap(raw_i1, "box")
    vert_perm = swap(perm, "grp")
    side_perm = swap(perm, "box")
    diag_perm = swap(side_perm, "grp")
    diag_raw = swap(side_raw, "grp")
    leaf, raw_i1 = lax.optimization_barrier((leaf, raw_i1))
    own_i1 = jnp.take(raw_i1, perm, axis=1, mode="clip")
    own_i2 = pick(leaf, perm[3 * width :], perm)
    own_ov = pick(leaf, perm[width : 3 * width], perm)
    side_i1 = jnp.take(side_raw, side_perm, axis=1, mode="clip")
    vert_i1 = jnp.take(vert_raw, vert_perm, axis=1, mode="clip")
    diag_i1 = jnp.take(diag_raw, diag_perm, axis=1, mode="clip")

    vert_i2 = swap(own_i2, "grp")
    bounds = [0, width // 2, 3 * width // 4, width]
    side_parts = []
    diag_parts = []
    after = side_raw
    for lo, hi in zip(bounds[:-1], bounds[1:]):
        part, after = lax.optimization_barrier((own_i2[lo:hi], after))
        landed = swap(part, "box")
        side_parts.append(landed)
        diag_parts.append(swap(landed, "grp"))
        after = landed
    side_i2 = jnp.concatenate(side_parts, 0)
    diag_i2 = jnp.concatenate(diag_parts, 0)

    solved_own = pair_solve(own_i1, side_i1, width)
    own_ext = first_rows(own_ov, solved_own, width)
    own_int = first_rows(own_i2, solved_own, width)
    side_int = second_rows(side_i2, solved_own, width)

    solved_other = pair_solve(vert_i1, diag_i1, width)
    vert_int = first_rows(vert_i2, solved_other, width)
    diag_int = second_rows(diag_i2, solved_other, width)

    near = jnp.concatenate([own_int, side_int], 0)
    far = jnp.concatenate([vert_int, diag_int], 0)
    system_two = int_cols(near, width) + int_cols(far, width)
    inverse_two = newton(system_two, ITERS_HIGH, matmul_high)
    weights = matmul_high(int_cols(own_ext, width), inverse_two)
    own_id = 2 * upper + right
    pieces = [
        own_ext[:, 0 : 2 * width] - matmul_high(weights, near[:, 0 : 2 * width]),
        own_ext[:, 3 * width : 5 * width] - matmul_high(weights, near[:, 3 * width : 5 * width]),
        -matmul_high(weights, far[:, 0 : 2 * width]),
        -matmul_high(weights, far[:, 3 * width : 5 * width]),
    ]
    merged = jnp.zeros((2 * width, 8 * width), jnp.float32)
    for rel, piece in enumerate(pieces):
        start = jnp.bitwise_xor(own_id, rel) * (2 * width)
        merged = lax.dynamic_update_slice(merged, piece, (0, start))
    return merged[None, None]


def solution(mesh):
    in_specs = (P("grp", "box", None, None), P("grp", "box", None, None))
    out_specs = P("grp", "box", None, None)
    return jax.shard_map(body, mesh=mesh, in_specs=in_specs, out_specs=out_specs, check_vma=False)
```

```python
import jax
import jax.numpy as jnp
from jax import lax
from jax.sharding import PartitionSpec as P

ITERS_LOW = 3
ITERS_HIGH = 3


def matmul(left, right):
    return jnp.dot(left, right, precision=lax.Precision.HIGHEST, preferred_element_type=jnp.float32)


def matmul_high(left, right):
    return jnp.dot(left, right, precision=lax.Precision.HIGH, preferred_element_type=jnp.float32)


def newton(system, steps, product=matmul):
    size = system.shape[0]
    eye = jnp.eye(size, dtype=jnp.float32)
    recip = 1.0 / jnp.sum(jnp.where(eye > 0, system, 0.0), axis=1)
    inverse = 2.0 * eye * recip[None, :] - recip[:, None] * system * recip[None, :]
    for sweep_index in range(steps - 1):
        inverse = 2.0 * inverse - product(product(inverse, system), inverse)
    return inverse


def swap(value, axis):
    size = lax.axis_size(axis)
    half = size // 2
    pairs = [(source, (source + half) % size) for source in range(size)]
    return lax.ppermute(value, axis, pairs)


def pair_solve(inverse, first_ie, second_ie):
    return -matmul(inverse, jnp.concatenate([first_ie, second_ie], 1))


def first_rows(rows, solved, width):
    blank = jnp.zeros((rows.shape[0], 3 * width), jnp.float32)
    return jnp.concatenate([rows[:, width:], blank], 1) + matmul(rows[:, :width], solved)


def second_rows(rows, solved, width):
    blank = jnp.zeros((rows.shape[0], 3 * width), jnp.float32)
    return jnp.concatenate([blank, rows[:, width:]], 1) + matmul(rows[:, :width], solved)


def ext_cols(parent, width):
    return jnp.concatenate(
        [parent[:, 0 : 2 * width], parent[:, 3 * width : 5 * width]], 1
    )


def int_cols(parent, width):
    return jnp.concatenate(
        [parent[:, 2 * width : 3 * width], parent[:, 5 * width : 6 * width]], 1
    )


def pick(matrix, rows, cols):
    picked = jnp.take(matrix, rows, axis=0, mode="clip")
    return jnp.take(picked, cols, axis=1, mode="clip")


def body(leaf_maps, side_points):
    upper = lax.axis_index("grp") // (lax.axis_size("grp") // 2)
    right = lax.axis_index("box") // (lax.axis_size("box") // 2)
    leaf = leaf_maps[0, 0]
    side_lists = side_points[0, 0]
    width = side_lists.shape[1]
    order = jnp.stack([1 - right, right, 2 + upper, 3 - upper])
    perm = jnp.take(side_lists, order, axis=0, mode="clip").reshape(4 * width)
    own_i1 = pick(leaf, perm[:width], perm)
    leaf, own_i1 = lax.optimization_barrier((leaf, own_i1))
    own_i2 = pick(leaf, perm[3 * width :], perm)
    own_ov = pick(leaf, perm[width : 3 * width], perm)

    half = width // 2
    vert_ie = swap(own_i1[:, width:], "grp")
    vert_i2 = swap(own_i2, "grp")
    side_i1 = swap(own_i1, "box")
    diag_ie = swap(side_i1[:, width:], "grp")
    inverse_own = newton(own_i1[:, :width] + side_i1[:, :width], ITERS_LOW)
    inverse_other = swap(inverse_own, "grp")
    first_half, side_i1 = lax.optimization_barrier((own_i2[:half], side_i1))
    side_first = swap(first_half, "box")
    diag_first = swap(side_first, "grp")
    second_half, side_first = lax.optimization_barrier((own_i2[half:], side_first))
    side_second = swap(second_half, "box")
    diag_second = swap(side_second, "grp")
    side_i2 = jnp.concatenate([side_first, side_second], 0)
    diag_i2 = jnp.concatenate([diag_first, diag_second], 0)

    solved_own = pair_solve(inverse_own, own_i1[:, width:], side_i1[:, width:])
    own_ext = first_rows(own_ov, solved_own, width)
    own_int = first_rows(own_i2, solved_own, width)
    side_int = second_rows(side_i2, solved_own, width)

    solved_other = pair_solve(inverse_other, vert_ie, diag_ie)
    vert_int = first_rows(vert_i2, solved_other, width)
    diag_int = second_rows(diag_i2, solved_other, width)

    near = jnp.concatenate([own_int, side_int], 0)
    far = jnp.concatenate([vert_int, diag_int], 0)
    system_two = int_cols(near, width) + int_cols(far, width)
    inverse_two = newton(system_two, ITERS_HIGH, matmul_high)
    weights = matmul_high(int_cols(own_ext, width), inverse_two)
    own_id = 2 * upper + right
    pieces = [
        own_ext[:, 0 : 2 * width] - matmul_high(weights, near[:, 0 : 2 * width]),
        own_ext[:, 3 * width : 5 * width] - matmul_high(weights, near[:, 3 * width : 5 * width]),
        -matmul_high(weights, far[:, 0 : 2 * width]),
        -matmul_high(weights, far[:, 3 * width : 5 * width]),
    ]
    merged = jnp.zeros((2 * width, 8 * width), jnp.float32)
    for rel, piece in enumerate(pieces):
        start = jnp.bitwise_xor(own_id, rel) * (2 * width)
        merged = lax.dynamic_update_slice(merged, piece, (0, start))
    return merged[None, None]


def solution(mesh):
    in_specs = (P("grp", "box", None, None), P("grp", "box", None, None))
    out_specs = P("grp", "box", None, None)
    return jax.shard_map(body, mesh=mesh, in_specs=in_specs, out_specs=out_specs, check_vma=False)
```

```python
import jax
import jax.numpy as jnp
from jax import lax
from jax.sharding import PartitionSpec as P

ITERS_LOW = 3
ITERS_HIGH = 3


def matmul(left, right):
    return jnp.dot(left, right, precision=lax.Precision.HIGHEST, preferred_element_type=jnp.float32)


def matmul_high(left, right):
    return jnp.dot(left, right, precision=lax.Precision.HIGH, preferred_element_type=jnp.float32)


def newton(system, steps, product=matmul):
    size = system.shape[0]
    eye = jnp.eye(size, dtype=jnp.float32)
    recip = 1.0 / jnp.sum(jnp.where(eye > 0, system, 0.0), axis=1)
    inverse = 2.0 * eye * recip[None, :] - recip[:, None] * system * recip[None, :]
    for sweep_index in range(steps - 1):
        inverse = 2.0 * inverse - product(product(inverse, system), inverse)
    return inverse


def swap(value, axis):
    size = lax.axis_size(axis)
    half = size // 2
    pairs = [(source, (source + half) % size) for source in range(size)]
    return lax.ppermute(value, axis, pairs)


def pair_solve(inverse, first_ie, second_ie):
    return -matmul(inverse, jnp.concatenate([first_ie, second_ie], 1))


def first_rows(rows, solved, width):
    blank = jnp.zeros((rows.shape[0], 3 * width), jnp.float32)
    return jnp.concatenate([rows[:, width:], blank], 1) + matmul(rows[:, :width], solved)


def second_rows(rows, solved, width):
    blank = jnp.zeros((rows.shape[0], 3 * width), jnp.float32)
    return jnp.concatenate([blank, rows[:, width:]], 1) + matmul(rows[:, :width], solved)


def ext_cols(parent, width):
    return jnp.concatenate(
        [parent[:, 0 : 2 * width], parent[:, 3 * width : 5 * width]], 1
    )


def int_cols(parent, width):
    return jnp.concatenate(
        [parent[:, 2 * width : 3 * width], parent[:, 5 * width : 6 * width]], 1
    )


def pick(matrix, rows, cols):
    picked = jnp.take(matrix, rows, axis=0, mode="clip")
    return jnp.take(picked, cols, axis=1, mode="clip")


def body(leaf_maps, side_points):
    upper = lax.axis_index("grp") // (lax.axis_size("grp") // 2)
    right = lax.axis_index("box") // (lax.axis_size("box") // 2)
    leaf = leaf_maps[0, 0]
    side_lists = side_points[0, 0]
    width = side_lists.shape[1]
    order = jnp.stack([1 - right, right, 2 + upper, 3 - upper])
    perm = jnp.take(side_lists, order, axis=0, mode="clip").reshape(4 * width)
    own_i1 = pick(leaf, perm[:width], perm)
    leaf, own_i1 = lax.optimization_barrier((leaf, own_i1))
    own_i2 = pick(leaf, perm[3 * width :], perm)
    own_ov = pick(leaf, perm[width : 3 * width], perm)

    vert_ie = swap(own_i1[:, width:], "grp")
    vert_i2 = swap(own_i2, "grp")
    side_i1 = swap(own_i1, "box")
    diag_ie = swap(side_i1[:, width:], "grp")
    inverse_own = newton(own_i1[:, :width] + side_i1[:, :width], ITERS_LOW)
    inverse_other = swap(inverse_own, "grp")
    bounds = [0, width // 2, 3 * width // 4, width]
    side_parts = []
    diag_parts = []
    after = side_i1
    for lo, hi in zip(bounds[:-1], bounds[1:]):
        part, after = lax.optimization_barrier((own_i2[lo:hi], after))
        landed = swap(part, "box")
        side_parts.append(landed)
        diag_parts.append(swap(landed, "grp"))
        after = landed
    side_i2 = jnp.concatenate(side_parts, 0)
    diag_i2 = jnp.concatenate(diag_parts, 0)

    solved_own = pair_solve(inverse_own, own_i1[:, width:], side_i1[:, width:])
    own_ext = first_rows(own_ov, solved_own, width)
    own_int = first_rows(own_i2, solved_own, width)
    side_int = second_rows(side_i2, solved_own, width)

    solved_other = pair_solve(inverse_other, vert_ie, diag_ie)
    vert_int = first_rows(vert_i2, solved_other, width)
    diag_int = second_rows(diag_i2, solved_other, width)

    near = jnp.concatenate([own_int, side_int], 0)
    far = jnp.concatenate([vert_int, diag_int], 0)
    system_two = int_cols(near, width) + int_cols(far, width)
    inverse_two = newton(system_two, ITERS_HIGH, matmul_high)
    weights = matmul_high(int_cols(own_ext, width), inverse_two)
    own_id = 2 * upper + right
    pieces = [
        own_ext[:, 0 : 2 * width] - matmul_high(weights, near[:, 0 : 2 * width]),
        own_ext[:, 3 * width : 5 * width] - matmul_high(weights, near[:, 3 * width : 5 * width]),
        -matmul_high(weights, far[:, 0 : 2 * width]),
        -matmul_high(weights, far[:, 3 * width : 5 * width]),
    ]
    merged = jnp.zeros((2 * width, 8 * width), jnp.float32)
    for rel, piece in enumerate(pieces):
        start = jnp.bitwise_xor(own_id, rel) * (2 * width)
        merged = lax.dynamic_update_slice(merged, piece, (0, start))
    return merged[None, None]


def solution(mesh):
    in_specs = (P("grp", "box", None, None), P("grp", "box", None, None))
    out_specs = P("grp", "box", None, None)
    return jax.shard_map(body, mesh=mesh, in_specs=in_specs, out_specs=out_specs, check_vma=False)
```

```python
import jax
import jax.numpy as jnp
from jax import lax
from jax.sharding import PartitionSpec as P

ITERS_LOW = 3
ITERS_HIGH = 3


def matmul(left, right):
    return jnp.dot(left, right, precision=lax.Precision.HIGHEST, preferred_element_type=jnp.float32)


def matmul_high(left, right):
    return jnp.dot(left, right, precision=lax.Precision.HIGH, preferred_element_type=jnp.float32)


def newton(system, steps, product=matmul):
    size = system.shape[0]
    eye = jnp.eye(size, dtype=jnp.float32)
    recip = 1.0 / jnp.sum(jnp.where(eye > 0, system, 0.0), axis=1)
    inverse = 2.0 * eye * recip[None, :] - recip[:, None] * system * recip[None, :]
    for sweep_index in range(steps - 1):
        inverse = 2.0 * inverse - product(product(inverse, system), inverse)
    return inverse


def swap(value, axis):
    size = lax.axis_size(axis)
    half = size // 2
    pairs = [(source, (source + half) % size) for source in range(size)]
    return lax.ppermute(value, axis, pairs)


def pair_solve(inverse, first_ie, second_ie):
    return -matmul(inverse, jnp.concatenate([first_ie, second_ie], 1))


def first_rows(rows, solved, width):
    blank = jnp.zeros((rows.shape[0], 3 * width), jnp.float32)
    return jnp.concatenate([rows[:, width:], blank], 1) + matmul(rows[:, :width], solved)


def second_rows(rows, solved, width):
    blank = jnp.zeros((rows.shape[0], 3 * width), jnp.float32)
    return jnp.concatenate([blank, rows[:, width:]], 1) + matmul(rows[:, :width], solved)


def ext_cols(parent, width):
    return jnp.concatenate(
        [parent[:, 0 : 2 * width], parent[:, 3 * width : 5 * width]], 1
    )


def int_cols(parent, width):
    return jnp.concatenate(
        [parent[:, 2 * width : 3 * width], parent[:, 5 * width : 6 * width]], 1
    )


def pick(matrix, rows, cols):
    picked = jnp.take(matrix, rows, axis=0, mode="clip")
    return jnp.take(picked, cols, axis=1, mode="clip")


def body(leaf_maps, side_points):
    upper = lax.axis_index("grp") // (lax.axis_size("grp") // 2)
    right = lax.axis_index("box") // (lax.axis_size("box") // 2)
    leaf = leaf_maps[0, 0]
    side_lists = side_points[0, 0]
    width = side_lists.shape[1]
    order = jnp.stack([1 - right, right, 2 + upper, 3 - upper])
    perm = jnp.take(side_lists, order, axis=0, mode="clip").reshape(4 * width)
    rows_i1 = jnp.take(leaf, perm[:width], axis=0, mode="clip")
    own_ii = jnp.take(rows_i1, perm[:width], axis=1, mode="clip")
    own_ie = jnp.take(rows_i1, perm[width:], axis=1, mode="clip")
    leaf, own_ii, own_ie = lax.optimization_barrier((leaf, own_ii, own_ie))
    own_i2 = pick(leaf, perm[3 * width :], perm)
    own_ov = pick(leaf, perm[width : 3 * width], perm)

    half = width // 2
    vert_ie = swap(own_ie, "grp")
    vert_i2 = swap(own_i2, "grp")
    side_ii = swap(own_ii, "box")
    side_ie = swap(own_ie, "box")
    diag_ie = swap(side_ie, "grp")
    inverse_own = newton(own_ii + side_ii, ITERS_LOW)
    inverse_other = swap(inverse_own, "grp")
    first_half, side_ie = lax.optimization_barrier((own_i2[:half], side_ie))
    side_first = swap(first_half, "box")
    diag_first = swap(side_first, "grp")
    second_half, side_first = lax.optimization_barrier((own_i2[half:], side_first))
    side_second = swap(second_half, "box")
    diag_second = swap(side_second, "grp")
    side_i2 = jnp.concatenate([side_first, side_second], 0)
    diag_i2 = jnp.concatenate([diag_first, diag_second], 0)

    solved_own = pair_solve(inverse_own, own_ie, side_ie)
    own_ext = first_rows(own_ov, solved_own, width)
    own_int = first_rows(own_i2, solved_own, width)
    side_int = second_rows(side_i2, solved_own, width)

    solved_other = pair_solve(inverse_other, vert_ie, diag_ie)
    vert_int = first_rows(vert_i2, solved_other, width)
    diag_int = second_rows(diag_i2, solved_other, width)

    near = jnp.concatenate([own_int, side_int], 0)
    far = jnp.concatenate([vert_int, diag_int], 0)
    system_two = int_cols(near, width) + int_cols(far, width)
    inverse_two = newton(system_two, ITERS_HIGH, matmul_high)
    weights = matmul_high(int_cols(own_ext, width), inverse_two)
    own_id = 2 * upper + right
    pieces = [
        own_ext[:, 0 : 2 * width] - matmul_high(weights, near[:, 0 : 2 * width]),
        own_ext[:, 3 * width : 5 * width] - matmul_high(weights, near[:, 3 * width : 5 * width]),
        -matmul_high(weights, far[:, 0 : 2 * width]),
        -matmul_high(weights, far[:, 3 * width : 5 * width]),
    ]
    merged = jnp.zeros((2 * width, 8 * width), jnp.float32)
    for rel, piece in enumerate(pieces):
        start = jnp.bitwise_xor(own_id, rel) * (2 * width)
        merged = lax.dynamic_update_slice(merged, piece, (0, start))
    return merged[None, None]


def solution(mesh):
    in_specs = (P("grp", "box", None, None), P("grp", "box", None, None))
    out_specs = P("grp", "box", None, None)
    return jax.shard_map(body, mesh=mesh, in_specs=in_specs, out_specs=out_specs, check_vma=False)
```

```python
import jax
import jax.numpy as jnp
from jax import lax
from jax.sharding import PartitionSpec as P

ITERS_LOW = 3
ITERS_HIGH = 3


def matmul(left, right):
    return jnp.dot(left, right, precision=lax.Precision.HIGHEST, preferred_element_type=jnp.float32)


def matmul_high(left, right):
    return jnp.dot(left, right, precision=lax.Precision.HIGH, preferred_element_type=jnp.float32)


def newton(system, steps, product=matmul):
    size = system.shape[0]
    eye = jnp.eye(size, dtype=jnp.float32)
    recip = 1.0 / jnp.sum(jnp.where(eye > 0, system, 0.0), axis=1)
    inverse = 2.0 * eye * recip[None, :] - recip[:, None] * system * recip[None, :]
    for sweep_index in range(steps - 1):
        inverse = 2.0 * inverse - product(product(inverse, system), inverse)
    return inverse


def swap(value, axis):
    size = lax.axis_size(axis)
    half = size // 2
    pairs = [(source, (source + half) % size) for source in range(size)]
    return lax.ppermute(value, axis, pairs)


def pair_solve(inverse, first_ie, second_ie, product=matmul):
    return -product(inverse, jnp.concatenate([first_ie, second_ie], 1))


def first_rows(rows, solved, width, product=matmul):
    blank = jnp.zeros((rows.shape[0], 3 * width), jnp.float32)
    return jnp.concatenate([rows[:, width:], blank], 1) + product(rows[:, :width], solved)


def second_rows(rows, solved, width, product=matmul):
    blank = jnp.zeros((rows.shape[0], 3 * width), jnp.float32)
    return jnp.concatenate([blank, rows[:, width:]], 1) + product(rows[:, :width], solved)


def ext_cols(parent, width):
    return jnp.concatenate(
        [parent[:, 0 : 2 * width], parent[:, 3 * width : 5 * width]], 1
    )


def int_cols(parent, width):
    return jnp.concatenate(
        [parent[:, 2 * width : 3 * width], parent[:, 5 * width : 6 * width]], 1
    )


def pick(matrix, rows, cols):
    picked = jnp.take(matrix, rows, axis=0, mode="clip")
    return jnp.take(picked, cols, axis=1, mode="clip")


def body(leaf_maps, side_points):
    upper = lax.axis_index("grp") // (lax.axis_size("grp") // 2)
    right = lax.axis_index("box") // (lax.axis_size("box") // 2)
    leaf = leaf_maps[0, 0]
    side_lists = side_points[0, 0]
    width = side_lists.shape[1]
    order = jnp.stack([1 - right, right, 2 + upper, 3 - upper])
    perm = jnp.take(side_lists, order, axis=0, mode="clip").reshape(4 * width)
    own_i1 = pick(leaf, perm[:width], perm)
    leaf, own_i1 = lax.optimization_barrier((leaf, own_i1))
    own_i2 = pick(leaf, perm[3 * width :], perm)
    own_ov = pick(leaf, perm[width : 3 * width], perm)

    half = width // 2
    vert_ie = swap(own_i1[:, width:], "grp")
    vert_i2 = swap(own_i2, "grp")
    side_i1 = swap(own_i1, "box")
    diag_ie = swap(side_i1[:, width:], "grp")
    inverse_own = newton(own_i1[:, :width] + side_i1[:, :width], ITERS_LOW)
    inverse_other = swap(inverse_own, "grp")
    first_half, side_i1 = lax.optimization_barrier((own_i2[:half], side_i1))
    side_first = swap(first_half, "box")
    diag_first = swap(side_first, "grp")
    second_half, side_first = lax.optimization_barrier((own_i2[half:], side_first))
    side_second = swap(second_half, "box")
    diag_second = swap(side_second, "grp")
    side_i2 = jnp.concatenate([side_first, side_second], 0)
    diag_i2 = jnp.concatenate([diag_first, diag_second], 0)

    solved_own = pair_solve(inverse_own, own_i1[:, width:], side_i1[:, width:])
    own_ext = first_rows(own_ov, solved_own, width)
    own_int = first_rows(own_i2, solved_own, width)
    side_int = second_rows(side_i2, solved_own, width)

    solved_other = pair_solve(inverse_other, vert_ie, diag_ie, matmul_high)
    vert_int = first_rows(vert_i2, solved_other, width, matmul_high)
    diag_int = second_rows(diag_i2, solved_other, width, matmul_high)

    near = jnp.concatenate([own_int, side_int], 0)
    far = jnp.concatenate([vert_int, diag_int], 0)
    system_two = int_cols(near, width) + int_cols(far, width)
    inverse_two = newton(system_two, ITERS_HIGH, matmul_high)
    weights = matmul_high(int_cols(own_ext, width), inverse_two)
    own_id = 2 * upper + right
    blocks = [
        near[:, 0 : 2 * width],
        near[:, 3 * width : 5 * width],
        far[:, 0 : 2 * width],
        far[:, 3 * width : 5 * width],
    ]
    coupling_two = jnp.zeros((2 * width, 8 * width), jnp.float32)
    for rel, block in enumerate(blocks):
        start = jnp.bitwise_xor(own_id, rel) * (2 * width)
        coupling_two = lax.dynamic_update_slice(coupling_two, block, (0, start))
    own_block = jnp.zeros((2 * width, 8 * width), jnp.float32)
    own_block = lax.dynamic_update_slice(own_block, own_ext[:, 0 : 2 * width], (0, own_id * (2 * width)))
    mate_start = jnp.bitwise_xor(own_id, 1) * (2 * width)
    own_block = lax.dynamic_update_slice(own_block, own_ext[:, 3 * width : 5 * width], (0, mate_start))
    merged = own_block - matmul_high(weights, coupling_two)
    return merged[None, None]


def solution(mesh):
    in_specs = (P("grp", "box", None, None), P("grp", "box", None, None))
    out_specs = P("grp", "box", None, None)
    return jax.shard_map(body, mesh=mesh, in_specs=in_specs, out_specs=out_specs, check_vma=False)
```

```python
import jax
import jax.numpy as jnp
from jax import lax
from jax.sharding import PartitionSpec as P

ITERS_LOW = 3
ITERS_HIGH = 3


def matmul(left, right):
    return jnp.dot(left, right, precision=lax.Precision.HIGHEST, preferred_element_type=jnp.float32)


def matmul_high(left, right):
    return jnp.dot(left, right, precision=lax.Precision.HIGH, preferred_element_type=jnp.float32)


def newton(system, steps, product=matmul):
    size = system.shape[0]
    eye = jnp.eye(size, dtype=jnp.float32)
    recip = 1.0 / jnp.sum(jnp.where(eye > 0, system, 0.0), axis=1)
    inverse = 2.0 * eye * recip[None, :] - recip[:, None] * system * recip[None, :]
    for sweep_index in range(steps - 1):
        inverse = 2.0 * inverse - product(product(inverse, system), inverse)
    return inverse


def swap(value, axis):
    size = lax.axis_size(axis)
    half = size // 2
    pairs = [(source, (source + half) % size) for source in range(size)]
    return lax.ppermute(value, axis, pairs)


def pair_solve(inverse, first_ie, second_ie, product=matmul):
    return -product(inverse, jnp.concatenate([first_ie, second_ie], 1))


def first_rows(rows, solved, width, product=matmul):
    blank = jnp.zeros((rows.shape[0], 3 * width), jnp.float32)
    return jnp.concatenate([rows[:, width:], blank], 1) + product(rows[:, :width], solved)


def second_rows(rows, solved, width, product=matmul):
    blank = jnp.zeros((rows.shape[0], 3 * width), jnp.float32)
    return jnp.concatenate([blank, rows[:, width:]], 1) + product(rows[:, :width], solved)


def ext_cols(parent, width):
    return jnp.concatenate(
        [parent[:, 0 : 2 * width], parent[:, 3 * width : 5 * width]], 1
    )


def int_cols(parent, width):
    return jnp.concatenate(
        [parent[:, 2 * width : 3 * width], parent[:, 5 * width : 6 * width]], 1
    )


def select_cols(rows, cols):
    size = rows.shape[1]
    chooser = (jnp.arange(size, dtype=jnp.int32)[:, None] == cols[None, :]).astype(jnp.bfloat16)
    high = lax.reduce_precision(rows, exponent_bits=8, mantissa_bits=7)
    rest = rows - high
    middle = lax.reduce_precision(rest, exponent_bits=8, mantissa_bits=7)
    low = rest - middle
    parts = [
        jnp.dot(part.astype(jnp.bfloat16), chooser, preferred_element_type=jnp.float32)
        for part in (high, middle, low)
    ]
    return (parts[0] + parts[1]) + parts[2]


def pick(matrix, rows, cols):
    picked = jnp.take(matrix, rows, axis=0, mode="clip")
    return jnp.take(picked, cols, axis=1, mode="clip")


def body(leaf_maps, side_points):
    upper = lax.axis_index("grp") // (lax.axis_size("grp") // 2)
    right = lax.axis_index("box") // (lax.axis_size("box") // 2)
    leaf = leaf_maps[0, 0]
    side_lists = side_points[0, 0]
    width = side_lists.shape[1]
    order = jnp.stack([1 - right, right, 2 + upper, 3 - upper])
    perm = jnp.take(side_lists, order, axis=0, mode="clip").reshape(4 * width)
    rows_i1 = jnp.take(leaf, perm[:width], axis=0, mode="clip")
    own_i1 = select_cols(rows_i1, perm)
    own_ie = select_cols(rows_i1, perm[width:])
    leaf, own_i1, own_ie = lax.optimization_barrier((leaf, own_i1, own_ie))
    own_i2 = pick(leaf, perm[3 * width :], perm)
    own_ov = pick(leaf, perm[width : 3 * width], perm)

    half = width // 2
    vert_ie = swap(own_ie, "grp")
    vert_i2 = swap(own_i2, "grp")
    side_i1 = swap(own_i1, "box")
    diag_ie = swap(side_i1[:, width:], "grp")
    inverse_own = newton(own_i1[:, :width] + side_i1[:, :width], ITERS_LOW)
    inverse_other = swap(inverse_own, "grp")
    first_half, side_i1 = lax.optimization_barrier((own_i2[:half], side_i1))
    side_first = swap(first_half, "box")
    diag_first = swap(side_first, "grp")
    second_half, side_first = lax.optimization_barrier((own_i2[half:], side_first))
    side_second = swap(second_half, "box")
    diag_second = swap(side_second, "grp")
    side_i2 = jnp.concatenate([side_first, side_second], 0)
    diag_i2 = jnp.concatenate([diag_first, diag_second], 0)

    solved_own = pair_solve(inverse_own, own_ie, side_i1[:, width:])
    own_ext = first_rows(own_ov, solved_own, width)
    own_int = first_rows(own_i2, solved_own, width)
    side_int = second_rows(side_i2, solved_own, width)

    solved_other = pair_solve(inverse_other, vert_ie, diag_ie, matmul_high)
    vert_int = first_rows(vert_i2, solved_other, width, matmul_high)
    diag_int = second_rows(diag_i2, solved_other, width, matmul_high)

    near = jnp.concatenate([own_int, side_int], 0)
    far = jnp.concatenate([vert_int, diag_int], 0)
    system_two = int_cols(near, width) + int_cols(far, width)
    inverse_two = newton(system_two, ITERS_HIGH, matmul_high)
    weights = matmul_high(int_cols(own_ext, width), inverse_two)
    own_id = 2 * upper + right
    blocks = [
        near[:, 0 : 2 * width],
        near[:, 3 * width : 5 * width],
        far[:, 0 : 2 * width],
        far[:, 3 * width : 5 * width],
    ]
    coupling_two = jnp.zeros((2 * width, 8 * width), jnp.float32)
    for rel, block in enumerate(blocks):
        start = jnp.bitwise_xor(own_id, rel) * (2 * width)
        coupling_two = lax.dynamic_update_slice(coupling_two, block, (0, start))
    own_block = jnp.zeros((2 * width, 8 * width), jnp.float32)
    own_block = lax.dynamic_update_slice(own_block, own_ext[:, 0 : 2 * width], (0, own_id * (2 * width)))
    mate_start = jnp.bitwise_xor(own_id, 1) * (2 * width)
    own_block = lax.dynamic_update_slice(own_block, own_ext[:, 3 * width : 5 * width], (0, mate_start))
    merged = own_block - matmul_high(weights, coupling_two)
    return merged[None, None]


def solution(mesh):
    in_specs = (P("grp", "box", None, None), P("grp", "box", None, None))
    out_specs = P("grp", "box", None, None)
    return jax.shard_map(body, mesh=mesh, in_specs=in_specs, out_specs=out_specs, check_vma=False)
```

```python
import jax
import jax.numpy as jnp
from jax import lax
from jax.sharding import PartitionSpec as P

ITERS_LOW = 3
ITERS_HIGH = 3


def matmul(left, right):
    return jnp.dot(left, right, precision=lax.Precision.HIGHEST, preferred_element_type=jnp.float32)


def matmul_high(left, right):
    return jnp.dot(left, right, precision=lax.Precision.HIGH, preferred_element_type=jnp.float32)


def newton(system, steps, product=matmul):
    size = system.shape[0]
    eye = jnp.eye(size, dtype=jnp.float32)
    recip = 1.0 / jnp.sum(jnp.where(eye > 0, system, 0.0), axis=1)
    inverse = 2.0 * eye * recip[None, :] - recip[:, None] * system * recip[None, :]
    for sweep_index in range(steps - 1):
        inverse = 2.0 * inverse - product(product(inverse, system), inverse)
    return inverse


def swap(value, axis):
    size = lax.axis_size(axis)
    half = size // 2
    pairs = [(source, (source + half) % size) for source in range(size)]
    return lax.ppermute(value, axis, pairs)


def pair_solve(inverse, first_ie, second_ie, product=matmul):
    return -product(inverse, jnp.concatenate([first_ie, second_ie], 1))


def first_rows(rows, solved, width, product=matmul):
    blank = jnp.zeros((rows.shape[0], 3 * width), jnp.float32)
    return jnp.concatenate([rows[:, width:], blank], 1) + product(rows[:, :width], solved)


def second_rows(rows, solved, width, product=matmul):
    blank = jnp.zeros((rows.shape[0], 3 * width), jnp.float32)
    return jnp.concatenate([blank, rows[:, width:]], 1) + product(rows[:, :width], solved)


def ext_cols(parent, width):
    return jnp.concatenate(
        [parent[:, 0 : 2 * width], parent[:, 3 * width : 5 * width]], 1
    )


def int_cols(parent, width):
    return jnp.concatenate(
        [parent[:, 2 * width : 3 * width], parent[:, 5 * width : 6 * width]], 1
    )


def pick(matrix, rows, cols):
    picked = jnp.take(matrix, rows, axis=0, mode="clip")
    return jnp.take(picked, cols, axis=1, mode="clip")


def body(leaf_maps, side_points):
    upper = lax.axis_index("grp") // (lax.axis_size("grp") // 2)
    right = lax.axis_index("box") // (lax.axis_size("box") // 2)
    leaf = leaf_maps[0, 0]
    side_lists = side_points[0, 0]
    width = side_lists.shape[1]
    order = jnp.stack([1 - right, right, 2 + upper, 3 - upper])
    perm = jnp.take(side_lists, order, axis=0, mode="clip").reshape(4 * width)
    own_i1 = pick(leaf, perm[:width], perm)
    leaf, own_i1 = lax.optimization_barrier((leaf, own_i1))
    own_i2 = pick(leaf, perm[3 * width :], perm)
    own_ov = pick(leaf, perm[width : 3 * width], perm)

    half = width // 2
    vert_ie = swap(own_i1[:, width:], "grp")
    vert_i2 = swap(own_i2, "grp")
    side_i1 = swap(own_i1, "box")
    diag_ie = swap(side_i1[:, width:], "grp")
    inverse_own = newton(own_i1[:, :width] + side_i1[:, :width], ITERS_LOW)
    inverse_other = swap(inverse_own, "grp")
    own_a = jnp.concatenate([own_i2[:, :width], own_i2[:, 3 * width :]], 1)
    part_a, side_i1 = lax.optimization_barrier((own_a, side_i1))
    side_a = swap(part_a, "box")
    diag_a = swap(side_a, "grp")
    part_b, side_a = lax.optimization_barrier((own_i2[:, width : 3 * width], side_a))
    side_b = swap(part_b, "box")
    diag_b = swap(side_b, "grp")
    side_i2 = jnp.concatenate([side_a[:, :width], side_b, side_a[:, width:]], 1)

    solved_own = pair_solve(inverse_own, own_i1[:, width:], side_i1[:, width:])
    own_ext = first_rows(own_ov, solved_own, width)
    own_int = first_rows(own_i2, solved_own, width)
    side_int = second_rows(side_i2, solved_own, width)

    solved_other = pair_solve(inverse_other, vert_ie, diag_ie, matmul_high)
    vert_int = first_rows(vert_i2, solved_other, width, matmul_high)
    diag_prod = matmul_high(diag_a[:, :width], solved_other)
    diag_inner = jnp.concatenate(
        [diag_prod[:, 2 * width : 3 * width], diag_prod[:, 5 * width :] + diag_a[:, width:]], 1
    )

    near = jnp.concatenate([own_int, side_int], 0)
    far_int = jnp.concatenate([int_cols(vert_int, width), diag_inner], 0)
    system_two = int_cols(near, width) + far_int
    inverse_two = newton(system_two, ITERS_HIGH, matmul_high)
    weights = matmul_high(int_cols(own_ext, width), inverse_two)
    own_id = 2 * upper + right
    blocks = [
        near[:, 0 : 2 * width],
        near[:, 3 * width : 5 * width],
        jnp.concatenate([vert_int[:, 0 : 2 * width], diag_prod[:, 0 : 2 * width]], 0),
        jnp.concatenate(
            [vert_int[:, 3 * width : 5 * width], diag_prod[:, 3 * width : 5 * width] + diag_b], 0
        ),
    ]
    coupling_two = jnp.zeros((2 * width, 8 * width), jnp.float32)
    for rel, block in enumerate(blocks):
        start = jnp.bitwise_xor(own_id, rel) * (2 * width)
        coupling_two = lax.dynamic_update_slice(coupling_two, block, (0, start))
    own_block = jnp.zeros((2 * width, 8 * width), jnp.float32)
    own_block = lax.dynamic_update_slice(own_block, own_ext[:, 0 : 2 * width], (0, own_id * (2 * width)))
    mate_start = jnp.bitwise_xor(own_id, 1) * (2 * width)
    own_block = lax.dynamic_update_slice(own_block, own_ext[:, 3 * width : 5 * width], (0, mate_start))
    merged = own_block - matmul_high(weights, coupling_two)
    return merged[None, None]


def solution(mesh):
    in_specs = (P("grp", "box", None, None), P("grp", "box", None, None))
    out_specs = P("grp", "box", None, None)
    return jax.shard_map(body, mesh=mesh, in_specs=in_specs, out_specs=out_specs, check_vma=False)
```

```python
import jax
import jax.numpy as jnp
from jax import lax
from jax.sharding import PartitionSpec as P

ITERS_LOW = 3
ITERS_HIGH = 3


def matmul(left, right):
    return jnp.dot(left, right, precision=lax.Precision.HIGHEST, preferred_element_type=jnp.float32)


def matmul_high(left, right):
    return jnp.dot(left, right, precision=lax.Precision.HIGH, preferred_element_type=jnp.float32)


def newton(system, steps, product=matmul):
    size = system.shape[0]
    eye = jnp.eye(size, dtype=jnp.float32)
    recip = 1.0 / jnp.sum(jnp.where(eye > 0, system, 0.0), axis=1)
    inverse = 2.0 * eye * recip[None, :] - recip[:, None] * system * recip[None, :]
    for sweep_index in range(steps - 1):
        inverse = 2.0 * inverse - product(product(inverse, system), inverse)
    return inverse


def swap(value, axis):
    size = lax.axis_size(axis)
    half = size // 2
    pairs = [(source, (source + half) % size) for source in range(size)]
    return lax.ppermute(value, axis, pairs)


def pair_solve(inverse, first_ie, second_ie, product=matmul):
    return -product(inverse, jnp.concatenate([first_ie, second_ie], 1))


def first_rows(rows, solved, width, product=matmul):
    blank = jnp.zeros((rows.shape[0], 3 * width), jnp.float32)
    return jnp.concatenate([rows[:, width:], blank], 1) + product(rows[:, :width], solved)


def second_rows(rows, solved, width, product=matmul):
    blank = jnp.zeros((rows.shape[0], 3 * width), jnp.float32)
    return jnp.concatenate([blank, rows[:, width:]], 1) + product(rows[:, :width], solved)


def ext_cols(parent, width):
    return jnp.concatenate(
        [parent[:, 0 : 2 * width], parent[:, 3 * width : 5 * width]], 1
    )


def int_cols(parent, width):
    return jnp.concatenate(
        [parent[:, 2 * width : 3 * width], parent[:, 5 * width : 6 * width]], 1
    )


def pick(matrix, rows, cols):
    picked = jnp.take(matrix, rows, axis=0, mode="clip")
    return jnp.take(picked, cols, axis=1, mode="clip")


def body(leaf_maps, side_points):
    upper = lax.axis_index("grp") // (lax.axis_size("grp") // 2)
    right = lax.axis_index("box") // (lax.axis_size("box") // 2)
    leaf = leaf_maps[0, 0]
    side_lists = side_points[0, 0]
    width = side_lists.shape[1]
    order = jnp.stack([1 - right, right, 2 + upper, 3 - upper])
    perm = jnp.take(side_lists, order, axis=0, mode="clip").reshape(4 * width)
    own_i1 = pick(leaf, perm[:width], perm)
    leaf, own_i1 = lax.optimization_barrier((leaf, own_i1))
    own_i2 = pick(leaf, perm[3 * width :], perm)
    own_ov = pick(leaf, perm[width : 3 * width], perm)

    half = width // 2
    vert_ie = swap(own_i1[:, width:], "grp")
    vert_i2 = swap(own_i2, "grp")
    side_i1 = swap(own_i1, "box")
    diag_ie = swap(side_i1[:, width:], "grp")
    inverse_own = newton(own_i1[:, :width] + side_i1[:, :width], ITERS_LOW)
    inverse_other = swap(inverse_own, "grp")
    own_a = jnp.concatenate([own_i2[:, :width], own_i2[:, 3 * width :]], 1)
    part_a, side_i1 = lax.optimization_barrier((own_a, side_i1))
    side_a = swap(part_a, "box")
    diag_a = swap(side_a, "grp")
    part_b, side_a = lax.optimization_barrier((own_i2[:, width : 3 * width], side_a))
    side_b = swap(part_b, "box")
    side_i2 = jnp.concatenate([side_a[:, :width], side_b, side_a[:, width:]], 1)

    solved_own = pair_solve(inverse_own, own_i1[:, width:], side_i1[:, width:])
    own_ext = first_rows(own_ov, solved_own, width)
    own_int = first_rows(own_i2, solved_own, width)
    side_int = second_rows(side_i2, solved_own, width)

    solved_other = pair_solve(inverse_other, vert_ie, diag_ie, matmul_high)
    vert_int = first_rows(vert_i2, solved_other, width, matmul_high)
    diag_prod = matmul_high(diag_a[:, :width], solved_other)
    diag_inner = jnp.concatenate(
        [diag_prod[:, 2 * width : 3 * width], diag_prod[:, 5 * width :] + diag_a[:, width:]], 1
    )

    near = jnp.concatenate([own_int, side_int], 0)
    far_int = jnp.concatenate([int_cols(vert_int, width), diag_inner], 0)
    system_two = int_cols(near, width) + far_int
    system_two, side_b = lax.optimization_barrier((system_two, side_b))
    diag_b = swap(side_b, "grp")
    inverse_two = newton(system_two, ITERS_HIGH, matmul_high)
    weights = matmul_high(int_cols(own_ext, width), inverse_two)
    own_id = 2 * upper + right
    blocks = [
        near[:, 0 : 2 * width],
        near[:, 3 * width : 5 * width],
        jnp.concatenate([vert_int[:, 0 : 2 * width], diag_prod[:, 0 : 2 * width]], 0),
        jnp.concatenate(
            [vert_int[:, 3 * width : 5 * width], diag_prod[:, 3 * width : 5 * width] + diag_b], 0
        ),
    ]
    coupling_two = jnp.zeros((2 * width, 8 * width), jnp.float32)
    for rel, block in enumerate(blocks):
        start = jnp.bitwise_xor(own_id, rel) * (2 * width)
        coupling_two = lax.dynamic_update_slice(coupling_two, block, (0, start))
    own_block = jnp.zeros((2 * width, 8 * width), jnp.float32)
    own_block = lax.dynamic_update_slice(own_block, own_ext[:, 0 : 2 * width], (0, own_id * (2 * width)))
    mate_start = jnp.bitwise_xor(own_id, 1) * (2 * width)
    own_block = lax.dynamic_update_slice(own_block, own_ext[:, 3 * width : 5 * width], (0, mate_start))
    merged = own_block - matmul_high(weights, coupling_two)
    return merged[None, None]


def solution(mesh):
    in_specs = (P("grp", "box", None, None), P("grp", "box", None, None))
    out_specs = P("grp", "box", None, None)
    return jax.shard_map(body, mesh=mesh, in_specs=in_specs, out_specs=out_specs, check_vma=False)
```

```python
import jax
import jax.numpy as jnp
from jax import lax
from jax.sharding import PartitionSpec as P

ITERS_LOW = 3
ITERS_HIGH = 3


def matmul(left, right):
    return jnp.dot(left, right, precision=lax.Precision.HIGHEST, preferred_element_type=jnp.float32)


def matmul_high(left, right):
    return jnp.dot(left, right, precision=lax.Precision.HIGH, preferred_element_type=jnp.float32)


def newton(system, steps, product=matmul):
    size = system.shape[0]
    eye = jnp.eye(size, dtype=jnp.float32)
    recip = 1.0 / jnp.sum(jnp.where(eye > 0, system, 0.0), axis=1)
    inverse = 2.0 * eye * recip[None, :] - recip[:, None] * system * recip[None, :]
    for sweep_index in range(steps - 1):
        inverse = 2.0 * inverse - product(product(inverse, system), inverse)
    return inverse


def swap(value, axis):
    size = lax.axis_size(axis)
    half = size // 2
    pairs = [(source, (source + half) % size) for source in range(size)]
    return lax.ppermute(value, axis, pairs)


def pair_solve(inverse, first_ie, second_ie, product=matmul):
    return -product(inverse, jnp.concatenate([first_ie, second_ie], 1))


def first_rows(rows, solved, width, product=matmul):
    blank = jnp.zeros((rows.shape[0], 3 * width), jnp.float32)
    return jnp.concatenate([rows[:, width:], blank], 1) + product(rows[:, :width], solved)


def second_rows(rows, solved, width, product=matmul):
    blank = jnp.zeros((rows.shape[0], 3 * width), jnp.float32)
    return jnp.concatenate([blank, rows[:, width:]], 1) + product(rows[:, :width], solved)


def ext_cols(parent, width):
    return jnp.concatenate(
        [parent[:, 0 : 2 * width], parent[:, 3 * width : 5 * width]], 1
    )


def int_cols(parent, width):
    return jnp.concatenate(
        [parent[:, 2 * width : 3 * width], parent[:, 5 * width : 6 * width]], 1
    )


def pick(matrix, rows, cols):
    picked = jnp.take(matrix, rows, axis=0, mode="clip")
    return jnp.take(picked, cols, axis=1, mode="clip")


def body(leaf_maps, side_points):
    upper = lax.axis_index("grp") // (lax.axis_size("grp") // 2)
    right = lax.axis_index("box") // (lax.axis_size("box") // 2)
    leaf = leaf_maps[0, 0]
    side_lists = side_points[0, 0]
    width = side_lists.shape[1]
    order = jnp.stack([1 - right, right, 2 + upper, 3 - upper])
    perm = jnp.take(side_lists, order, axis=0, mode="clip").reshape(4 * width)
    own_i1 = pick(leaf, perm[:width], perm)
    leaf, own_i1 = lax.optimization_barrier((leaf, own_i1))
    own_i2 = pick(leaf, perm[3 * width :], perm)
    own_ov = pick(leaf, perm[width : 3 * width], perm)

    half = width // 2
    vert_ie = swap(own_i1[:, width:], "grp")
    vert_i2 = swap(own_i2, "grp")
    side_i1 = swap(own_i1, "box")
    diag_ie = swap(side_i1[:, width:], "grp")
    inverse_own = newton(own_i1[:, :width] + side_i1[:, :width], ITERS_LOW)
    inverse_other = swap(inverse_own, "grp")
    first_half, side_i1 = lax.optimization_barrier((own_i2[:half], side_i1))
    side_first = swap(first_half, "box")
    diag_first = swap(side_first, "grp")
    second_half, side_first = lax.optimization_barrier((own_i2[half:], side_first))
    side_second = swap(second_half, "box")
    diag_second = swap(side_second, "grp")
    side_i2 = jnp.concatenate([side_first, side_second], 0)
    diag_i2 = jnp.concatenate([diag_first, diag_second], 0)

    solved_own = pair_solve(inverse_own, own_i1[:, width:], side_i1[:, width:], matmul_high)
    own_ext = first_rows(own_ov, solved_own, width, matmul_high)
    own_int = first_rows(own_i2, solved_own, width, matmul_high)
    side_int = second_rows(side_i2, solved_own, width, matmul_high)

    solved_other = pair_solve(inverse_other, vert_ie, diag_ie, matmul_high)
    vert_int = first_rows(vert_i2, solved_other, width, matmul_high)
    diag_int = second_rows(diag_i2, solved_other, width, matmul_high)

    near = jnp.concatenate([own_int, side_int], 0)
    far = jnp.concatenate([vert_int, diag_int], 0)
    system_two = int_cols(near, width) + int_cols(far, width)
    inverse_two = newton(system_two, ITERS_HIGH, matmul_high)
    weights = matmul_high(int_cols(own_ext, width), inverse_two)
    own_id = 2 * upper + right
    blocks = [
        near[:, 0 : 2 * width],
        near[:, 3 * width : 5 * width],
        far[:, 0 : 2 * width],
        far[:, 3 * width : 5 * width],
    ]
    coupling_two = jnp.zeros((2 * width, 8 * width), jnp.float32)
    for rel, block in enumerate(blocks):
        start = jnp.bitwise_xor(own_id, rel) * (2 * width)
        coupling_two = lax.dynamic_update_slice(coupling_two, block, (0, start))
    own_block = jnp.zeros((2 * width, 8 * width), jnp.float32)
    own_block = lax.dynamic_update_slice(own_block, own_ext[:, 0 : 2 * width], (0, own_id * (2 * width)))
    mate_start = jnp.bitwise_xor(own_id, 1) * (2 * width)
    own_block = lax.dynamic_update_slice(own_block, own_ext[:, 3 * width : 5 * width], (0, mate_start))
    merged = own_block - matmul_high(weights, coupling_two)
    return merged[None, None]


def solution(mesh):
    in_specs = (P("grp", "box", None, None), P("grp", "box", None, None))
    out_specs = P("grp", "box", None, None)
    return jax.shard_map(body, mesh=mesh, in_specs=in_specs, out_specs=out_specs, check_vma=False)
```

```python
import jax
import jax.numpy as jnp
from jax import lax
from jax.sharding import PartitionSpec as P

ITERS_LOW = 3
ITERS_HIGH = 3


def matmul(left, right):
    return jnp.dot(left, right, precision=lax.Precision.HIGHEST, preferred_element_type=jnp.float32)


def matmul_high(left, right):
    return jnp.dot(left, right, precision=lax.Precision.HIGH, preferred_element_type=jnp.float32)


def newton(system, steps, product=matmul):
    size = system.shape[0]
    eye = jnp.eye(size, dtype=jnp.float32)
    recip = 1.0 / jnp.sum(jnp.where(eye > 0, system, 0.0), axis=1)
    inverse = 2.0 * eye * recip[None, :] - recip[:, None] * system * recip[None, :]
    for sweep_index in range(steps - 1):
        inverse = 2.0 * inverse - product(product(inverse, system), inverse)
    return inverse


def swap(value, axis):
    size = lax.axis_size(axis)
    half = size // 2
    pairs = [(source, (source + half) % size) for source in range(size)]
    return lax.ppermute(value, axis, pairs)


def pair_solve(inverse, first_ie, second_ie, product=matmul):
    return -product(inverse, jnp.concatenate([first_ie, second_ie], 1))


def first_rows(rows, solved, width, product=matmul):
    blank = jnp.zeros((rows.shape[0], 3 * width), jnp.float32)
    return jnp.concatenate([rows[:, width:], blank], 1) + product(rows[:, :width], solved)


def second_rows(rows, solved, width, product=matmul):
    blank = jnp.zeros((rows.shape[0], 3 * width), jnp.float32)
    return jnp.concatenate([blank, rows[:, width:]], 1) + product(rows[:, :width], solved)


def ext_cols(parent, width):
    return jnp.concatenate(
        [parent[:, 0 : 2 * width], parent[:, 3 * width : 5 * width]], 1
    )


def int_cols(parent, width):
    return jnp.concatenate(
        [parent[:, 2 * width : 3 * width], parent[:, 5 * width : 6 * width]], 1
    )


def pick(matrix, rows, cols):
    picked = jnp.take(matrix, rows, axis=0, mode="clip")
    return jnp.take(picked, cols, axis=1, mode="clip")


def body(leaf_maps, side_points):
    upper = lax.axis_index("grp") // (lax.axis_size("grp") // 2)
    right = lax.axis_index("box") // (lax.axis_size("box") // 2)
    leaf = leaf_maps[0, 0]
    side_lists = side_points[0, 0]
    width = side_lists.shape[1]
    order = jnp.stack([1 - right, right, 2 + upper, 3 - upper])
    perm = jnp.take(side_lists, order, axis=0, mode="clip").reshape(4 * width)
    own_i1 = pick(leaf, perm[:width], perm)
    leaf, own_i1 = lax.optimization_barrier((leaf, own_i1))
    own_i2 = pick(leaf, perm[3 * width :], perm)
    own_a = pick(leaf, perm[3 * width :], jnp.concatenate([perm[:width], perm[3 * width :]]))
    own_b = pick(leaf, perm[3 * width :], perm[width : 3 * width])
    own_ov = pick(leaf, perm[width : 3 * width], perm)

    vert_ie = swap(own_i1[:, width:], "grp")
    vert_i2 = swap(own_i2, "grp")
    side_i1 = swap(own_i1, "box")
    diag_ie = swap(side_i1[:, width:], "grp")
    inverse_own = newton(own_i1[:, :width] + side_i1[:, :width], ITERS_LOW)
    inverse_other = swap(inverse_own, "grp")
    part_a, side_i1 = lax.optimization_barrier((own_a, side_i1))
    side_a = swap(part_a, "box")
    diag_a = swap(side_a, "grp")
    part_b, side_a = lax.optimization_barrier((own_b, side_a))
    side_b = swap(part_b, "box")

    solved_own = pair_solve(inverse_own, own_i1[:, width:], side_i1[:, width:])
    own_ext = first_rows(own_ov, solved_own, width)
    own_int = first_rows(own_i2, solved_own, width)
    side_prod = matmul(side_a[:, :width], solved_own)
    side_inner = jnp.concatenate(
        [side_prod[:, 2 * width : 3 * width], side_prod[:, 5 * width :] + side_a[:, width:]], 1
    )

    solved_other = pair_solve(inverse_other, vert_ie, diag_ie, matmul_high)
    vert_int = first_rows(vert_i2, solved_other, width, matmul_high)
    diag_prod = matmul_high(diag_a[:, :width], solved_other)
    diag_inner = jnp.concatenate(
        [diag_prod[:, 2 * width : 3 * width], diag_prod[:, 5 * width :] + diag_a[:, width:]], 1
    )

    near_int = jnp.concatenate([int_cols(own_int, width), side_inner], 0)
    far_int = jnp.concatenate([int_cols(vert_int, width), diag_inner], 0)
    near_int, side_b = lax.optimization_barrier((near_int, side_b))
    diag_b = swap(side_b, "grp")
    system_two = near_int + far_int
    inverse_two = newton(system_two, ITERS_HIGH, matmul_high)
    weights = matmul_high(int_cols(own_ext, width), inverse_two)
    own_id = 2 * upper + right
    blocks = [
        jnp.concatenate([own_int[:, 0 : 2 * width], side_prod[:, 0 : 2 * width]], 0),
        jnp.concatenate(
            [own_int[:, 3 * width : 5 * width], side_prod[:, 3 * width : 5 * width] + side_b], 0
        ),
        jnp.concatenate([vert_int[:, 0 : 2 * width], diag_prod[:, 0 : 2 * width]], 0),
        jnp.concatenate(
            [vert_int[:, 3 * width : 5 * width], diag_prod[:, 3 * width : 5 * width] + diag_b], 0
        ),
    ]
    coupling_two = jnp.zeros((2 * width, 8 * width), jnp.float32)
    for rel, block in enumerate(blocks):
        start = jnp.bitwise_xor(own_id, rel) * (2 * width)
        coupling_two = lax.dynamic_update_slice(coupling_two, block, (0, start))
    own_block = jnp.zeros((2 * width, 8 * width), jnp.float32)
    own_block = lax.dynamic_update_slice(own_block, own_ext[:, 0 : 2 * width], (0, own_id * (2 * width)))
    mate_start = jnp.bitwise_xor(own_id, 1) * (2 * width)
    own_block = lax.dynamic_update_slice(own_block, own_ext[:, 3 * width : 5 * width], (0, mate_start))
    merged = own_block - matmul_high(weights, coupling_two)
    return merged[None, None]


def solution(mesh):
    in_specs = (P("grp", "box", None, None), P("grp", "box", None, None))
    out_specs = P("grp", "box", None, None)
    return jax.shard_map(body, mesh=mesh, in_specs=in_specs, out_specs=out_specs, check_vma=False)
```

```python
import jax
import jax.numpy as jnp
from jax import lax
from jax.sharding import PartitionSpec as P

ITERS_LOW = 3
ITERS_HIGH = 3


def matmul(left, right):
    return jnp.dot(left, right, precision=lax.Precision.HIGHEST, preferred_element_type=jnp.float32)


def matmul_high(left, right):
    return jnp.dot(left, right, precision=lax.Precision.HIGH, preferred_element_type=jnp.float32)


def newton(system, steps, product=matmul):
    size = system.shape[0]
    eye = jnp.eye(size, dtype=jnp.float32)
    recip = 1.0 / jnp.sum(jnp.where(eye > 0, system, 0.0), axis=1)
    inverse = 2.0 * eye * recip[None, :] - recip[:, None] * system * recip[None, :]
    for sweep_index in range(steps - 1):
        inverse = 2.0 * inverse - product(product(inverse, system), inverse)
    return inverse


def swap(value, axis):
    size = lax.axis_size(axis)
    half = size // 2
    pairs = [(source, (source + half) % size) for source in range(size)]
    return lax.ppermute(value, axis, pairs)


def pair_solve(inverse, first_ie, second_ie, product=matmul):
    return -product(inverse, jnp.concatenate([first_ie, second_ie], 1))


def first_rows(rows, solved, width, product=matmul):
    blank = jnp.zeros((rows.shape[0], 3 * width), jnp.float32)
    return jnp.concatenate([rows[:, width:], blank], 1) + product(rows[:, :width], solved)


def second_rows(rows, solved, width, product=matmul):
    blank = jnp.zeros((rows.shape[0], 3 * width), jnp.float32)
    return jnp.concatenate([blank, rows[:, width:]], 1) + product(rows[:, :width], solved)


def ext_cols(parent, width):
    return jnp.concatenate(
        [parent[:, 0 : 2 * width], parent[:, 3 * width : 5 * width]], 1
    )


def int_cols(parent, width):
    return jnp.concatenate(
        [parent[:, 2 * width : 3 * width], parent[:, 5 * width : 6 * width]], 1
    )


def pick(matrix, rows, cols):
    picked = jnp.take(matrix, rows, axis=0, mode="clip")
    return jnp.take(picked, cols, axis=1, mode="clip")


def body(leaf_maps, side_points):
    upper = lax.axis_index("grp") // (lax.axis_size("grp") // 2)
    right = lax.axis_index("box") // (lax.axis_size("box") // 2)
    leaf = leaf_maps[0, 0]
    side_lists = side_points[0, 0]
    width = side_lists.shape[1]
    order = jnp.stack([1 - right, right, 2 + upper, 3 - upper])
    perm = jnp.take(side_lists, order, axis=0, mode="clip").reshape(4 * width)
    own_i1 = pick(leaf, perm[:width], perm)
    leaf, own_i1 = lax.optimization_barrier((leaf, own_i1))
    own_i2 = pick(leaf, perm[3 * width :], perm)
    own_a = pick(leaf, perm[3 * width :], jnp.concatenate([perm[:width], perm[3 * width :]]))
    own_b = pick(leaf, perm[3 * width :], perm[width : 3 * width])
    own_ov = pick(leaf, perm[width : 3 * width], perm)

    vert_ie = swap(own_i1[:, width:], "grp")
    vert_i2 = swap(own_i2, "grp")
    side_i1 = swap(own_i1, "box")
    diag_ie = swap(side_i1[:, width:], "grp")
    inverse_own = newton(own_i1[:, :width] + side_i1[:, :width], ITERS_LOW)
    inverse_other = swap(inverse_own, "grp")
    part_a, side_i1 = lax.optimization_barrier((own_a, side_i1))
    side_a = swap(part_a, "box")
    diag_a = swap(side_a, "grp")
    part_b, side_a = lax.optimization_barrier((own_b, side_a))
    side_b = swap(part_b, "box")

    solved_own = pair_solve(inverse_own, own_i1[:, width:], side_i1[:, width:])
    own_ext = first_rows(own_ov, solved_own, width)
    own_int = first_rows(own_i2, solved_own, width)
    side_prod = matmul(side_a[:, :width], solved_own)
    side_inner = jnp.concatenate(
        [side_prod[:, 2 * width : 3 * width], side_prod[:, 5 * width :] + side_a[:, width:]], 1
    )

    solved_other = pair_solve(inverse_other, vert_ie, diag_ie, matmul_high)
    vert_int = first_rows(vert_i2, solved_other, width, matmul_high)
    diag_prod = matmul_high(diag_a[:, :width], solved_other)
    diag_inner = jnp.concatenate(
        [diag_prod[:, 2 * width : 3 * width], diag_prod[:, 5 * width :] + diag_a[:, width:]], 1
    )

    near_int = jnp.concatenate([int_cols(own_int, width), side_inner], 0)
    far_int = jnp.concatenate([int_cols(vert_int, width), diag_inner], 0)
    near_int, side_b = lax.optimization_barrier((near_int, side_b))
    diag_b = swap(side_b, "grp")
    system_two = near_int + far_int
    inverse_two = newton(system_two, ITERS_HIGH, matmul_high)
    weights = matmul_high(int_cols(own_ext, width), inverse_two)
    own_id = 2 * upper + right
    blocks = [
        jnp.concatenate([own_int[:, 0 : 2 * width], side_prod[:, 0 : 2 * width]], 0),
        jnp.concatenate(
            [own_int[:, 3 * width : 5 * width], side_prod[:, 3 * width : 5 * width] + side_b], 0
        ),
        jnp.concatenate([vert_int[:, 0 : 2 * width], diag_prod[:, 0 : 2 * width]], 0),
        jnp.concatenate(
            [vert_int[:, 3 * width : 5 * width], diag_prod[:, 3 * width : 5 * width] + diag_b], 0
        ),
    ]
    coupling_two = jnp.zeros((2 * width, 8 * width), jnp.float32)
    for rel, block in enumerate(blocks[:3]):
        start = jnp.bitwise_xor(own_id, rel) * (2 * width)
        coupling_two = lax.dynamic_update_slice(coupling_two, block, (0, start))
    own_block = jnp.zeros((2 * width, 8 * width), jnp.float32)
    own_block = lax.dynamic_update_slice(own_block, own_ext[:, 0 : 2 * width], (0, own_id * (2 * width)))
    mate_start = jnp.bitwise_xor(own_id, 1) * (2 * width)
    own_block = lax.dynamic_update_slice(own_block, own_ext[:, 3 * width : 5 * width], (0, mate_start))
    merged = own_block - matmul_high(weights, coupling_two)
    merged, diag_b = lax.optimization_barrier((merged, diag_b))
    blocks[3] = jnp.concatenate(
        [vert_int[:, 3 * width : 5 * width], diag_prod[:, 3 * width : 5 * width] + diag_b], 0
    )
    last_start = jnp.bitwise_xor(own_id, 3) * (2 * width)
    merged = lax.dynamic_update_slice(merged, -matmul_high(weights, blocks[3]), (0, last_start))
    return merged[None, None]


def solution(mesh):
    in_specs = (P("grp", "box", None, None), P("grp", "box", None, None))
    out_specs = P("grp", "box", None, None)
    return jax.shard_map(body, mesh=mesh, in_specs=in_specs, out_specs=out_specs, check_vma=False)
```

```python
import jax
import jax.numpy as jnp
from jax import lax
from jax.sharding import PartitionSpec as P

ITERS_LOW = 3
ITERS_HIGH = 3


def matmul(left, right):
    return jnp.dot(left, right, precision=lax.Precision.HIGHEST, preferred_element_type=jnp.float32)


def matmul_high(left, right):
    return jnp.dot(left, right, precision=lax.Precision.HIGH, preferred_element_type=jnp.float32)


def newton(system, steps, product=matmul):
    size = system.shape[0]
    eye = jnp.eye(size, dtype=jnp.float32)
    recip = 1.0 / jnp.sum(jnp.where(eye > 0, system, 0.0), axis=1)
    inverse = 2.0 * eye * recip[None, :] - recip[:, None] * system * recip[None, :]
    for sweep_index in range(steps - 1):
        inverse = 2.0 * inverse - product(product(inverse, system), inverse)
    return inverse


def swap(value, axis):
    size = lax.axis_size(axis)
    half = size // 2
    pairs = [(source, (source + half) % size) for source in range(size)]
    return lax.ppermute(value, axis, pairs)


def pair_solve(inverse, first_ie, second_ie, product=matmul):
    return -product(inverse, jnp.concatenate([first_ie, second_ie], 1))


def first_rows(rows, solved, width, product=matmul):
    blank = jnp.zeros((rows.shape[0], 3 * width), jnp.float32)
    return jnp.concatenate([rows[:, width:], blank], 1) + product(rows[:, :width], solved)


def second_rows(rows, solved, width, product=matmul):
    blank = jnp.zeros((rows.shape[0], 3 * width), jnp.float32)
    return jnp.concatenate([blank, rows[:, width:]], 1) + product(rows[:, :width], solved)


def ext_cols(parent, width):
    return jnp.concatenate(
        [parent[:, 0 : 2 * width], parent[:, 3 * width : 5 * width]], 1
    )


def int_cols(parent, width):
    return jnp.concatenate(
        [parent[:, 2 * width : 3 * width], parent[:, 5 * width : 6 * width]], 1
    )


def pick(matrix, rows, cols):
    picked = jnp.take(matrix, rows, axis=0, mode="clip")
    return jnp.take(picked, cols, axis=1, mode="clip")


def body(leaf_maps, side_points):
    upper = lax.axis_index("grp") // (lax.axis_size("grp") // 2)
    right = lax.axis_index("box") // (lax.axis_size("box") // 2)
    leaf = leaf_maps[0, 0]
    side_lists = side_points[0, 0]
    width = side_lists.shape[1]
    order = jnp.stack([1 - right, right, 2 + upper, 3 - upper])
    perm = jnp.take(side_lists, order, axis=0, mode="clip").reshape(4 * width)
    own_i1 = pick(leaf, perm[:width], perm)
    leaf, own_i1 = lax.optimization_barrier((leaf, own_i1))
    own_i2 = pick(leaf, perm[3 * width :], perm)
    own_a = pick(leaf, perm[3 * width :], jnp.concatenate([perm[:width], perm[3 * width :]]))
    own_b = pick(leaf, perm[3 * width :], perm[width : 3 * width])
    own_ov = pick(leaf, perm[width : 3 * width], perm)

    vert_ie = swap(own_i1[:, width:], "grp")
    vert_i2 = swap(own_i2, "grp")
    side_i1 = swap(own_i1, "box")
    diag_ie = swap(side_i1[:, width:], "grp")
    inverse_own = newton(own_i1[:, :width] + side_i1[:, :width], ITERS_LOW)
    inverse_other = swap(inverse_own, "grp")
    part_a, side_i1 = lax.optimization_barrier((own_a, side_i1))
    side_a = swap(part_a, "box")
    diag_a = swap(side_a, "grp")
    part_b, side_a = lax.optimization_barrier((own_b, side_a))
    side_b = swap(part_b, "box")

    solved_own = pair_solve(inverse_own, own_i1[:, width:], side_i1[:, width:])
    own_ext = first_rows(own_ov, solved_own, width)
    own_int = first_rows(own_i2, solved_own, width)
    side_prod = matmul(side_a[:, :width], solved_own)
    side_inner = jnp.concatenate(
        [side_prod[:, 2 * width : 3 * width], side_prod[:, 5 * width :] + side_a[:, width:]], 1
    )

    solved_other = pair_solve(inverse_other, vert_ie, diag_ie, matmul_high)
    vert_int = first_rows(vert_i2, solved_other, width, matmul_high)
    diag_prod = matmul_high(diag_a[:, :width], solved_other)
    diag_inner = jnp.concatenate(
        [diag_prod[:, 2 * width : 3 * width], diag_prod[:, 5 * width :] + diag_a[:, width:]], 1
    )

    near_int = jnp.concatenate([int_cols(own_int, width), side_inner], 0)
    far_int = jnp.concatenate([int_cols(vert_int, width), diag_inner], 0)
    near_int, side_b = lax.optimization_barrier((near_int, side_b))
    diag_b = swap(side_b, "grp")
    system_two = near_int + far_int
    inverse_two = newton(system_two, ITERS_HIGH, matmul_high)
    weights = matmul_high(int_cols(own_ext, width), inverse_two)
    own_id = 2 * upper + right
    blocks = [
        jnp.concatenate([own_int[:, 0 : 2 * width], side_prod[:, 0 : 2 * width]], 0),
        jnp.concatenate(
            [own_int[:, 3 * width : 5 * width], side_prod[:, 3 * width : 5 * width] + side_b], 0
        ),
        jnp.concatenate([vert_int[:, 0 : 2 * width], diag_prod[:, 0 : 2 * width]], 0),
        jnp.concatenate(
            [vert_int[:, 3 * width : 5 * width], diag_prod[:, 3 * width : 5 * width] + diag_b], 0
        ),
    ]
    first_three = matmul_high(weights, jnp.concatenate(blocks[:3], 1))
    own_parts = [own_ext[:, 0 : 2 * width], own_ext[:, 3 * width : 5 * width], None]
    merged = jnp.zeros((2 * width, 8 * width), jnp.float32)
    for rel, own_part in enumerate(own_parts):
        piece = -first_three[:, rel * 2 * width : (rel + 1) * 2 * width]
        if own_part is not None:
            piece = own_part + piece
        start = jnp.bitwise_xor(own_id, rel) * (2 * width)
        merged = lax.dynamic_update_slice(merged, piece, (0, start))
    merged, diag_b = lax.optimization_barrier((merged, diag_b))
    blocks[3] = jnp.concatenate(
        [vert_int[:, 3 * width : 5 * width], diag_prod[:, 3 * width : 5 * width] + diag_b], 0
    )
    last_start = jnp.bitwise_xor(own_id, 3) * (2 * width)
    merged = lax.dynamic_update_slice(merged, -matmul_high(weights, blocks[3]), (0, last_start))
    return merged[None, None]


def solution(mesh):
    in_specs = (P("grp", "box", None, None), P("grp", "box", None, None))
    out_specs = P("grp", "box", None, None)
    return jax.shard_map(body, mesh=mesh, in_specs=in_specs, out_specs=out_specs, check_vma=False)
```

```python
import jax
import jax.numpy as jnp
from jax import lax
from jax.sharding import PartitionSpec as P

ITERS_LOW = 3
ITERS_HIGH = 3


def matmul(left, right):
    return jnp.dot(left, right, precision=lax.Precision.HIGHEST, preferred_element_type=jnp.float32)


def matmul_high(left, right):
    return jnp.dot(left, right, precision=lax.Precision.HIGH, preferred_element_type=jnp.float32)


def newton(system, steps, product=matmul):
    size = system.shape[0]
    eye = jnp.eye(size, dtype=jnp.float32)
    recip = 1.0 / jnp.sum(jnp.where(eye > 0, system, 0.0), axis=1)
    inverse = 2.0 * eye * recip[None, :] - recip[:, None] * system * recip[None, :]
    for sweep_index in range(steps - 1):
        inverse = 2.0 * inverse - product(product(inverse, system), inverse)
    return inverse


def swap(value, axis):
    size = lax.axis_size(axis)
    half = size // 2
    pairs = [(source, (source + half) % size) for source in range(size)]
    return lax.ppermute(value, axis, pairs)


def pair_solve(inverse, first_ie, second_ie, product=matmul):
    return -product(inverse, jnp.concatenate([first_ie, second_ie], 1))


def first_rows(rows, solved, width, product=matmul):
    blank = jnp.zeros((rows.shape[0], 3 * width), jnp.float32)
    return jnp.concatenate([rows[:, width:], blank], 1) + product(rows[:, :width], solved)


def second_rows(rows, solved, width, product=matmul):
    blank = jnp.zeros((rows.shape[0], 3 * width), jnp.float32)
    return jnp.concatenate([blank, rows[:, width:]], 1) + product(rows[:, :width], solved)


def ext_cols(parent, width):
    return jnp.concatenate(
        [parent[:, 0 : 2 * width], parent[:, 3 * width : 5 * width]], 1
    )


def int_cols(parent, width):
    return jnp.concatenate(
        [parent[:, 2 * width : 3 * width], parent[:, 5 * width : 6 * width]], 1
    )


def pick(matrix, rows, cols):
    picked = jnp.take(matrix, rows, axis=0, mode="clip")
    return jnp.take(picked, cols, axis=1, mode="clip")


def body(leaf_maps, side_points):
    upper = lax.axis_index("grp") // (lax.axis_size("grp") // 2)
    right = lax.axis_index("box") // (lax.axis_size("box") // 2)
    leaf = leaf_maps[0, 0]
    side_lists = side_points[0, 0]
    width = side_lists.shape[1]
    order = jnp.stack([1 - right, right, 2 + upper, 3 - upper])
    perm = jnp.take(side_lists, order, axis=0, mode="clip").reshape(4 * width)
    own_i1 = pick(leaf, perm[:width], perm)
    leaf, own_i1 = lax.optimization_barrier((leaf, own_i1))
    own_i2 = pick(leaf, perm[3 * width :], perm)
    split_order = jnp.concatenate([perm[:width], perm[3 * width :], perm[width : 3 * width]])
    own_split = pick(leaf, perm[3 * width :], split_order)
    own_a = own_split[:, : 2 * width]
    own_b = own_split[:, 2 * width :]
    own_ov = pick(leaf, perm[width : 3 * width], perm)

    vert_ie = swap(own_i1[:, width:], "grp")
    vert_i2 = swap(own_i2, "grp")
    side_i1 = swap(own_i1, "box")
    diag_ie = swap(side_i1[:, width:], "grp")
    system_own = own_i1[:, :width] + side_i1[:, :width]
    inverse_other = newton(swap(system_own, "grp"), ITERS_LOW)
    inverse_own = newton(system_own, ITERS_LOW)
    part_a, side_i1 = lax.optimization_barrier((own_a, side_i1))
    side_a = swap(part_a, "box")
    diag_a = swap(side_a, "grp")
    part_b, side_a = lax.optimization_barrier((own_b, side_a))
    side_b = swap(part_b, "box")

    solved_own = pair_solve(inverse_own, own_i1[:, width:], side_i1[:, width:])
    own_ext = first_rows(own_ov, solved_own, width)
    own_int = first_rows(own_i2, solved_own, width)
    side_prod = matmul(side_a[:, :width], solved_own)
    side_inner = jnp.concatenate(
        [side_prod[:, 2 * width : 3 * width], side_prod[:, 5 * width :] + side_a[:, width:]], 1
    )

    solved_other = pair_solve(inverse_other, vert_ie, diag_ie, matmul_high)
    vert_int = first_rows(vert_i2, solved_other, width, matmul_high)
    diag_prod = matmul_high(diag_a[:, :width], solved_other)
    diag_inner = jnp.concatenate(
        [diag_prod[:, 2 * width : 3 * width], diag_prod[:, 5 * width :] + diag_a[:, width:]], 1
    )

    near_int = jnp.concatenate([int_cols(own_int, width), side_inner], 0)
    far_int = jnp.concatenate([int_cols(vert_int, width), diag_inner], 0)
    near_int, side_b = lax.optimization_barrier((near_int, side_b))
    diag_b = swap(side_b, "grp")
    system_two = near_int + far_int
    inverse_two = newton(system_two, ITERS_HIGH, matmul_high)
    weights = matmul_high(int_cols(own_ext, width), inverse_two)
    own_id = 2 * upper + right
    blocks = [
        jnp.concatenate([own_int[:, 0 : 2 * width], side_prod[:, 0 : 2 * width]], 0),
        jnp.concatenate(
            [own_int[:, 3 * width : 5 * width], side_prod[:, 3 * width : 5 * width] + side_b], 0
        ),
        jnp.concatenate([vert_int[:, 0 : 2 * width], diag_prod[:, 0 : 2 * width]], 0),
        jnp.concatenate(
            [vert_int[:, 3 * width : 5 * width], diag_prod[:, 3 * width : 5 * width] + diag_b], 0
        ),
    ]
    coupling_two = jnp.zeros((2 * width, 8 * width), jnp.float32)
    for rel, block in enumerate(blocks[:3]):
        start = jnp.bitwise_xor(own_id, rel) * (2 * width)
        coupling_two = lax.dynamic_update_slice(coupling_two, block, (0, start))
    own_block = jnp.zeros((2 * width, 8 * width), jnp.float32)
    own_block = lax.dynamic_update_slice(own_block, own_ext[:, 0 : 2 * width], (0, own_id * (2 * width)))
    mate_start = jnp.bitwise_xor(own_id, 1) * (2 * width)
    own_block = lax.dynamic_update_slice(own_block, own_ext[:, 3 * width : 5 * width], (0, mate_start))
    merged = own_block - matmul_high(weights, coupling_two)
    merged, diag_b = lax.optimization_barrier((merged, diag_b))
    blocks[3] = jnp.concatenate(
        [vert_int[:, 3 * width : 5 * width], diag_prod[:, 3 * width : 5 * width] + diag_b], 0
    )
    last_start = jnp.bitwise_xor(own_id, 3) * (2 * width)
    merged = lax.dynamic_update_slice(merged, -matmul_high(weights, blocks[3]), (0, last_start))
    return merged[None, None]


def solution(mesh):
    in_specs = (P("grp", "box", None, None), P("grp", "box", None, None))
    out_specs = P("grp", "box", None, None)
    return jax.shard_map(body, mesh=mesh, in_specs=in_specs, out_specs=out_specs, check_vma=False)
```

```python
import jax
import jax.numpy as jnp
from jax import lax
from jax.sharding import PartitionSpec as P

ITERS_LOW = 3
ITERS_HIGH = 3


def matmul(left, right):
    return jnp.dot(left, right, precision=lax.Precision.HIGHEST, preferred_element_type=jnp.float32)


def matmul_high(left, right):
    return jnp.dot(left, right, precision=lax.Precision.HIGH, preferred_element_type=jnp.float32)


def newton(system, steps, product=matmul):
    size = system.shape[0]
    eye = jnp.eye(size, dtype=jnp.float32)
    recip = 1.0 / jnp.sum(jnp.where(eye > 0, system, 0.0), axis=1)
    inverse = 2.0 * eye * recip[None, :] - recip[:, None] * system * recip[None, :]
    for sweep_index in range(steps - 1):
        inverse = 2.0 * inverse - product(product(inverse, system), inverse)
    return inverse


def swap(value, axis):
    size = lax.axis_size(axis)
    half = size // 2
    pairs = [(source, (source + half) % size) for source in range(size)]
    return lax.ppermute(value, axis, pairs)


def pair_solve(inverse, first_ie, second_ie, product=matmul):
    return -product(inverse, jnp.concatenate([first_ie, second_ie], 1))


def first_rows(rows, solved, width, product=matmul):
    blank = jnp.zeros((rows.shape[0], 3 * width), jnp.float32)
    return jnp.concatenate([rows[:, width:], blank], 1) + product(rows[:, :width], solved)


def second_rows(rows, solved, width, product=matmul):
    blank = jnp.zeros((rows.shape[0], 3 * width), jnp.float32)
    return jnp.concatenate([blank, rows[:, width:]], 1) + product(rows[:, :width], solved)


def ext_cols(parent, width):
    return jnp.concatenate(
        [parent[:, 0 : 2 * width], parent[:, 3 * width : 5 * width]], 1
    )


def int_cols(parent, width):
    return jnp.concatenate(
        [parent[:, 2 * width : 3 * width], parent[:, 5 * width : 6 * width]], 1
    )


def pick(matrix, rows, cols):
    picked = jnp.take(matrix, rows, axis=0, mode="clip")
    return jnp.take(picked, cols, axis=1, mode="clip")


def body(leaf_maps, side_points):
    upper = lax.axis_index("grp") // (lax.axis_size("grp") // 2)
    right = lax.axis_index("box") // (lax.axis_size("box") // 2)
    leaf = leaf_maps[0, 0]
    side_lists = side_points[0, 0]
    width = side_lists.shape[1]
    order = jnp.stack([1 - right, right, 2 + upper, 3 - upper])
    perm = jnp.take(side_lists, order, axis=0, mode="clip").reshape(4 * width)
    own_i1 = pick(leaf, perm[:width], perm)
    leaf, own_i1 = lax.optimization_barrier((leaf, own_i1))
    own_i2 = pick(leaf, perm[3 * width :], perm)
    own_a = pick(leaf, perm[3 * width :], jnp.concatenate([perm[:width], perm[3 * width :]]))
    own_b = pick(leaf, perm[3 * width :], perm[width : 3 * width])
    own_ov = pick(leaf, perm[width : 3 * width], perm)

    vert_ie = swap(own_i1[:, width:], "grp")
    vert_i2 = swap(own_i2, "grp")
    side_i1 = swap(own_i1, "box")
    diag_ie = swap(side_i1[:, width:], "grp")
    inverse_own = newton(own_i1[:, :width] + side_i1[:, :width], ITERS_LOW, matmul_high)
    inverse_other = swap(inverse_own, "grp")
    part_a, side_i1 = lax.optimization_barrier((own_a, side_i1))
    side_a = swap(part_a, "box")
    diag_a = swap(side_a, "grp")
    part_b, side_a = lax.optimization_barrier((own_b, side_a))
    side_b = swap(part_b, "box")

    solved_own = pair_solve(inverse_own, own_i1[:, width:], side_i1[:, width:])
    own_ext = first_rows(own_ov, solved_own, width)
    own_int = first_rows(own_i2, solved_own, width)
    side_prod = matmul(side_a[:, :width], solved_own)
    side_inner = jnp.concatenate(
        [side_prod[:, 2 * width : 3 * width], side_prod[:, 5 * width :] + side_a[:, width:]], 1
    )

    solved_other = pair_solve(inverse_other, vert_ie, diag_ie, matmul_high)
    vert_int = first_rows(vert_i2, solved_other, width, matmul_high)
    diag_prod = matmul_high(diag_a[:, :width], solved_other)
    diag_inner = jnp.concatenate(
        [diag_prod[:, 2 * width : 3 * width], diag_prod[:, 5 * width :] + diag_a[:, width:]], 1
    )

    near_int = jnp.concatenate([int_cols(own_int, width), side_inner], 0)
    far_int = jnp.concatenate([int_cols(vert_int, width), diag_inner], 0)
    near_int, side_b = lax.optimization_barrier((near_int, side_b))
    diag_b = swap(side_b, "grp")
    system_two = near_int + far_int
    inverse_two = newton(system_two, ITERS_HIGH, matmul_high)
    weights = matmul_high(int_cols(own_ext, width), inverse_two)
    own_id = 2 * upper + right
    blocks = [
        jnp.concatenate([own_int[:, 0 : 2 * width], side_prod[:, 0 : 2 * width]], 0),
        jnp.concatenate(
            [own_int[:, 3 * width : 5 * width], side_prod[:, 3 * width : 5 * width] + side_b], 0
        ),
        jnp.concatenate([vert_int[:, 0 : 2 * width], diag_prod[:, 0 : 2 * width]], 0),
        jnp.concatenate(
            [vert_int[:, 3 * width : 5 * width], diag_prod[:, 3 * width : 5 * width] + diag_b], 0
        ),
    ]
    coupling_two = jnp.zeros((2 * width, 8 * width), jnp.float32)
    for rel, block in enumerate(blocks[:3]):
        start = jnp.bitwise_xor(own_id, rel) * (2 * width)
        coupling_two = lax.dynamic_update_slice(coupling_two, block, (0, start))
    own_block = jnp.zeros((2 * width, 8 * width), jnp.float32)
    own_block = lax.dynamic_update_slice(own_block, own_ext[:, 0 : 2 * width], (0, own_id * (2 * width)))
    mate_start = jnp.bitwise_xor(own_id, 1) * (2 * width)
    own_block = lax.dynamic_update_slice(own_block, own_ext[:, 3 * width : 5 * width], (0, mate_start))
    merged = own_block - matmul_high(weights, coupling_two)
    merged, diag_b = lax.optimization_barrier((merged, diag_b))
    blocks[3] = jnp.concatenate(
        [vert_int[:, 3 * width : 5 * width], diag_prod[:, 3 * width : 5 * width] + diag_b], 0
    )
    last_start = jnp.bitwise_xor(own_id, 3) * (2 * width)
    merged = lax.dynamic_update_slice(merged, -matmul_high(weights, blocks[3]), (0, last_start))
    return merged[None, None]


def solution(mesh):
    in_specs = (P("grp", "box", None, None), P("grp", "box", None, None))
    out_specs = P("grp", "box", None, None)
    return jax.shard_map(body, mesh=mesh, in_specs=in_specs, out_specs=out_specs, check_vma=False)
```
